512 devices in a mesh: chan: 32 (over y, z_hi, core), tm: 16 (over x, z_lo).
Axes of the slice: x: 4, y: 8, z: 8 (z_hi: 2, z_lo: 4; z = z_hi * 4 + z_lo), core: 2. Of those that a mesh axis runs over, the one named last changes fastest.
Arguments:
- raw_records: bfloat16 [4096, 122880], P('chan', 'tm'), may hold values from -80 to 80
- keep_window: int32 [96], P('tm'), may hold values 0 or 1
Outputs:
- lag_stacks: bfloat16 [4096, 51, 256], P(('chan', 'tm'))
The draws below stay inside these ranges and needn't reach their ends.
All inputs are finite; a program needn't handle non-finite values. No bound on the sum of `keep_window` on one device may be relied on, other than what follows from the above.
Results may differ from the reference program's by a relative error of at most 0.018.
The reference program's roundings to bfloat16 on the way count: a program that leaves them out, or rounds other values in their place, can miss the bound.
Values may be sent and summed in bfloat16 or wider, within the bound.
No kernel may reach another device: no remote copies, remote signals or barrier semaphores. Data moves between devices by JAX's collectives and lax.ppermute only.
A program may use at most 64 MiB of HBM per device.

```python
import math
import jax
import jax.numpy as jnp
import numpy as np
from jax import lax

CH_DEV = 128
WIN_DEV = 6
W = 256
Q = 5
TAPS = 129
LAGS = 51
F = 128
RAWW = 1280
PAD = 128
CHANNELS = 4096
WINDOWS = 96
N_CHAN = 32
N_TM = 16


def draw_raw_records(key, part):
    total_len = WINDOWS * RAWW
    scale_key = jax.random.fold_in(key, 11)
    noise_key = jax.random.fold_in(key, 12)
    channel_scale = jnp.exp(jax.random.uniform(scale_key, (CHANNELS, 1), jnp.float32, 0.0, math.log(10.0)))
    innovation = jnp.clip(jax.random.normal(noise_key, (CHANNELS, total_len + 1), jnp.float32), -4.0, 4.0)
    coloured = innovation[:, 1:] - 0.95 * innovation[:, :-1]
    return (channel_scale * coloured).astype(jnp.bfloat16)


def place_ends(result, own_key, least, high):
    index_at = [jax.random.randint(jax.random.fold_in(own_key, axis), (), 0, length) for axis, length in enumerate(result.shape)]
    main_axis = result.shape.index(max(result.shape))
    neighbour = index_at[:main_axis] + [(index_at[main_axis] + 1) % result.shape[main_axis]] + index_at[main_axis + 1:]
    return result.at[tuple(index_at)].set(least).at[tuple(neighbour)].set(high)


def setup_inputs(seed: int = 0) -> dict:
    arg_keys = jax.random.split(jax.random.key(seed), 3)
    return {
        "raw_records": draw_raw_records(jax.random.fold_in(arg_keys[2], 71), 0),
        "keep_window": place_ends((jax.random.randint(arg_keys[1], (WINDOWS,), 0, 4) < 3).astype(jnp.int32), jax.random.fold_in(arg_keys[1], 1), 0, 1),
    }


def make_tables():
    tap_index = np.arange(TAPS)
    centre = (TAPS - 1) / 2.0
    hann_window = 0.5 - 0.5 * np.cos(2.0 * np.pi * (tap_index + 1) / (TAPS + 1))
    sinc_arg = 0.16 * (tap_index - centre)
    safe_arg = np.where(sinc_arg == 0.0, 1.0, sinc_arg)
    sinc_vals = np.where(sinc_arg == 0.0, 1.0, np.sin(np.pi * safe_arg) / (np.pi * safe_arg))
    fir_taps = sinc_vals * hann_window
    fir_taps = fir_taps / fir_taps.sum()
    sample = np.arange(W)
    bin_index = np.arange(F)
    phase_grid = 2.0 * np.pi * np.outer(sample, bin_index) / W
    dft_table = np.concatenate([np.cos(phase_grid), -np.sin(phase_grid)], axis=1)
    combined = np.zeros((PAD + RAWW, 2 * F))
    for tap_number in range(TAPS):
        row_index = Q * sample - tap_number + PAD
        combined[row_index] += fir_taps[tap_number] * dft_table
    rising = np.sin(0.5 * np.pi * np.minimum(1.0, bin_index / 10.0)) ** 2
    falling = np.sin(0.5 * np.pi * np.minimum(1.0, (F - bin_index) / 16.0)) ** 2
    band_taper = rising * falling
    lag_index = np.arange(LAGS) - (LAGS - 1) / 2.0
    lag_phase = 2.0 * np.pi * np.outer(bin_index, lag_index) / W
    weight = np.where(bin_index == 0, 1.0, 2.0)[:, None]
    lag_table = np.stack([weight * np.cos(lag_phase), weight * np.sin(lag_phase)])
    table_hist = jnp.asarray(combined[:PAD], jnp.float32).astype(jnp.bfloat16)
    table_main = jnp.asarray(combined[PAD:], jnp.float32).astype(jnp.bfloat16)
    return (table_hist, table_main, jnp.asarray(band_taper, jnp.float32), jnp.asarray(lag_table, jnp.float32).astype(jnp.bfloat16))

def whiten(spectrum, band_taper):
    amplitude = jnp.sqrt(spectrum[:, 0] * spectrum[:, 0] + spectrum[:, 1] * spectrum[:, 1])
    water_level = 0.5 * (lax.optimization_barrier(jnp.mean(amplitude, axis=1, keepdims=True)) + 1e-05)
    factor = band_taper[None, :, None] / jnp.maximum(amplitude, water_level)
    return lax.optimization_barrier((spectrum * factor[:, None]).astype(jnp.bfloat16))

def pair_term(own_rows, partner, lag_table):
    rotated = jnp.stack([own_rows[:, 1], -own_rows[:, 0]], axis=1)
    stacked_rows = jnp.stack([own_rows, rotated])
    cross_spec = jnp.einsum('qwpfi,wpfj->qfij', stacked_rows.astype(jnp.float32), partner.astype(jnp.float32))
    cross_spec = lax.optimization_barrier(cross_spec.astype(jnp.bfloat16))
    return jnp.einsum('pfij,pfl->ilj', cross_spec.astype(jnp.float32), lag_table.astype(jnp.float32))

def reference(raw_records, keep_window):
    table_hist, table_main, band_taper, lag_table = make_tables()
    lag_table = lax.optimization_barrier(lag_table)
    table_hist = lax.optimization_barrier(table_hist)
    table_main = lax.optimization_barrier(table_main)
    blocks = raw_records.reshape(N_CHAN, CH_DEV, WINDOWS, RAWW)

    def transform(raw_block):
        previous = jnp.concatenate([jnp.zeros((CH_DEV, 1, PAD), raw_block.dtype), raw_block[:, :-1, RAWW - PAD:]], axis=1)
        spectrum = jnp.einsum('cwr,rq->wqc', raw_block.astype(jnp.float32), table_main.astype(jnp.float32))
        spectrum = spectrum + jnp.einsum('cwr,rq->wqc', previous.astype(jnp.float32), table_hist.astype(jnp.float32))
        return whiten(spectrum.reshape(WINDOWS, 2, F, CH_DEV), band_taper)
    spectra = lax.map(transform, blocks)
    keep_weight = keep_window.astype(spectra.dtype)
    kept_all = spectra * keep_weight[None, :, None, None, None]
    norm_factor = 1.0 / math.sqrt(WINDOWS * F)

    def one_block(block_index):
        own_rows = kept_all[block_index].reshape(N_TM, WIN_DEV, 2, F, CH_DEV)
        partner_near = lax.dynamic_index_in_dim(spectra, (block_index + 1) % N_CHAN, 0, keepdims=False)
        partner_far = lax.dynamic_index_in_dim(spectra, (block_index + 2) % N_CHAN, 0, keepdims=False)
        partner_near = partner_near.reshape(N_TM, WIN_DEV, 2, F, CH_DEV)
        partner_far = partner_far.reshape(N_TM, WIN_DEV, 2, F, CH_DEV)

        def add_segment(running, pieces):
            segment_term = jnp.concatenate([pair_term(pieces[0], pieces[1], lag_table), pair_term(pieces[0], pieces[2], lag_table)], axis=2)
            rounded = lax.optimization_barrier(segment_term.astype(jnp.bfloat16))
            return (running + rounded.astype(jnp.float32), None)
        zero_stack = jnp.zeros((CH_DEV, LAGS, 2 * CH_DEV), jnp.float32)
        running, _ = lax.scan(add_segment, zero_stack, (own_rows, partner_near, partner_far))
        return (running * norm_factor).astype(jnp.bfloat16)
    stacks = lax.map(one_block, jnp.arange(N_CHAN, dtype=jnp.int32))
    return stacks.reshape(CHANNELS, LAGS, 2 * CH_DEV)
```

```python
import math

import jax
import jax.numpy as jnp
import numpy as np
from jax import lax
from jax.sharding import PartitionSpec as P

W = 256
Q = 5
TAPS = 129
LAGS = 51
F = 128
RAWW = 1280
PAD = 128


def passed_along(value, axis, by):
    devices = lax.axis_size(axis)
    pairs = [(i, i + by) for i in range(devices) if 0 <= i + by < devices]
    return lax.ppermute(value, axis, pairs)


def shifted(block, axis, distance):
    devices = range(lax.axis_size(axis))
    route = [((i - distance) % len(devices), i) for i in devices]
    return lax.ppermute(block, axis, route)


def make_tables():
    tap_index = np.arange(TAPS)
    centre = (TAPS - 1) / 2.0
    hann_window = 0.5 - 0.5 * np.cos(2.0 * np.pi * (tap_index + 1) / (TAPS + 1))
    sinc_arg = 0.16 * (tap_index - centre)
    safe_arg = np.where(sinc_arg == 0.0, 1.0, sinc_arg)
    sinc_vals = np.where(sinc_arg == 0.0, 1.0, np.sin(np.pi * safe_arg) / (np.pi * safe_arg))
    fir_taps = sinc_vals * hann_window
    fir_taps = fir_taps / fir_taps.sum()
    sample = np.arange(W)
    bin_index = np.arange(F)
    phase_grid = 2.0 * np.pi * np.outer(sample, bin_index) / W
    dft_table = np.concatenate([np.cos(phase_grid), -np.sin(phase_grid)], axis=1)
    combined = np.zeros((PAD + RAWW, 2 * F))
    for tap_number in range(TAPS):
        row_index = Q * sample - tap_number + PAD
        combined[row_index] += fir_taps[tap_number] * dft_table
    rising = np.sin(0.5 * np.pi * np.minimum(1.0, bin_index / 10.0)) ** 2
    falling = np.sin(0.5 * np.pi * np.minimum(1.0, (F - bin_index) / 16.0)) ** 2
    band_taper = rising * falling
    lag_index = np.arange(LAGS) - (LAGS - 1) / 2.0
    lag_phase = 2.0 * np.pi * np.outer(bin_index, lag_index) / W
    weight = np.where(bin_index == 0, 1.0, 2.0)[:, None]
    lag_table = np.stack([weight * np.cos(lag_phase), weight * np.sin(lag_phase)])
    table_hist = jnp.asarray(combined[:PAD], jnp.float32).astype(jnp.bfloat16)
    table_main = jnp.asarray(combined[PAD:], jnp.float32).astype(jnp.bfloat16)
    return (
        table_hist,
        table_main,
        jnp.asarray(band_taper, jnp.float32),
        jnp.asarray(lag_table, jnp.float32).astype(jnp.bfloat16),
    )


def whiten(spectrum, band_taper):
    amplitude = jnp.sqrt(spectrum[:, 0] * spectrum[:, 0] + spectrum[:, 1] * spectrum[:, 1])
    water_level = 0.5 * (jnp.mean(amplitude, axis=1, keepdims=True) + 1e-05)
    factor = band_taper[None, :, None] / jnp.maximum(amplitude, water_level)
    return (spectrum * factor[:, None]).astype(jnp.bfloat16)


def segment_terms(kept_spec, partner, lag_table):
    rotated = jnp.stack([kept_spec[:, 1], -kept_spec[:, 0]], axis=1)
    stacked_rows = jnp.stack([kept_spec, rotated])
    cross_spec = jnp.einsum(
        "qwpfi,wpfj->fqji", stacked_rows, partner, preferred_element_type=jnp.float32
    ).astype(jnp.bfloat16)
    rows, columns = kept_spec.shape[3], partner.shape[3]
    flat = cross_spec.reshape(2 * F, columns * rows)
    lag_flat = lag_table.transpose(1, 0, 2).reshape(2 * F, LAGS)
    terms = jnp.einsum("kn,kl->ln", flat, lag_flat, preferred_element_type=jnp.float32)
    return terms.astype(jnp.bfloat16).reshape(LAGS, columns, rows)


def per_device(raw_records, keep_window):
    channels_here = raw_records.shape[0]
    windows_here = keep_window.shape[0]
    segments = lax.axis_size("tm")
    table_hist, table_main, band_taper, lag_table = make_tables()
    blocked = raw_records.reshape(channels_here, windows_here, RAWW)
    history = passed_along(raw_records[:, windows_here * RAWW - PAD :], "tm", 1)
    previous = jnp.concatenate([history[:, None, :], blocked[:, :-1, RAWW - PAD :]], axis=1)
    spectrum = jnp.einsum("cwr,rq->wqc", blocked, table_main, preferred_element_type=jnp.float32)
    spectrum = spectrum + jnp.einsum(
        "cwr,rq->wqc", previous, table_hist, preferred_element_type=jnp.float32
    )
    whitened = whiten(spectrum.reshape(windows_here, 2, F, channels_here), band_taper)
    partner_near = shifted(whitened, "chan", -1)
    partner_far = shifted(whitened, "chan", -2)
    partner = jnp.concatenate([partner_near, partner_far], axis=3)
    kept_spec = whitened * keep_window.astype(jnp.bfloat16)[:, None, None, None]
    terms = segment_terms(kept_spec, partner, lag_table)
    row_count = channels_here // segments
    terms = terms.reshape(LAGS, partner.shape[3], segments, row_count).transpose(2, 3, 0, 1)
    gathered = lax.all_to_all(terms, "tm", 0, 0, tiled=True)
    stacked = jnp.sum(gathered.astype(jnp.float32), axis=0)
    norm_factor = 1.0 / math.sqrt(windows_here * segments * F)
    return (stacked * norm_factor).astype(jnp.bfloat16)


def solution(mesh):
    placed = (P("chan", "tm"), P("tm"))
    return jax.shard_map(
        per_device,
        mesh=mesh,
        in_specs=placed,
        out_specs=P(("chan", "tm"), None, None),
        check_vma=False,
    )
```

```python
import math

import jax
import jax.numpy as jnp
import numpy as np
from jax import lax
from jax.sharding import PartitionSpec as P

W = 256
Q = 5
TAPS = 129
LAGS = 51
F = 128
RAWW = 1280
PAD = 128


def passed_along(value, axis, by):
    devices = lax.axis_size(axis)
    pairs = [(i, i + by) for i in range(devices) if 0 <= i + by < devices]
    return lax.ppermute(value, axis, pairs)


def shifted(block, axis, distance):
    devices = range(lax.axis_size(axis))
    route = [((i - distance) % len(devices), i) for i in devices]
    return lax.ppermute(block, axis, route)


def make_tables():
    tap_index = np.arange(TAPS)
    centre = (TAPS - 1) / 2.0
    hann_window = 0.5 - 0.5 * np.cos(2.0 * np.pi * (tap_index + 1) / (TAPS + 1))
    sinc_arg = 0.16 * (tap_index - centre)
    safe_arg = np.where(sinc_arg == 0.0, 1.0, sinc_arg)
    sinc_vals = np.where(sinc_arg == 0.0, 1.0, np.sin(np.pi * safe_arg) / (np.pi * safe_arg))
    fir_taps = sinc_vals * hann_window
    fir_taps = fir_taps / fir_taps.sum()
    sample = np.arange(W)
    bin_index = np.arange(F)
    phase_grid = 2.0 * np.pi * np.outer(sample, bin_index) / W
    dft_table = np.concatenate([np.cos(phase_grid), -np.sin(phase_grid)], axis=1)
    combined = np.zeros((PAD + RAWW, 2 * F))
    for tap_number in range(TAPS):
        row_index = Q * sample - tap_number + PAD
        combined[row_index] += fir_taps[tap_number] * dft_table
    rising = np.sin(0.5 * np.pi * np.minimum(1.0, bin_index / 10.0)) ** 2
    falling = np.sin(0.5 * np.pi * np.minimum(1.0, (F - bin_index) / 16.0)) ** 2
    band_taper = rising * falling
    lag_index = np.arange(LAGS) - (LAGS - 1) / 2.0
    lag_phase = 2.0 * np.pi * np.outer(bin_index, lag_index) / W
    weight = np.where(bin_index == 0, 1.0, 2.0)[:, None]
    lag_table = np.stack([weight * np.cos(lag_phase), weight * np.sin(lag_phase)])
    table_hist = jnp.asarray(combined[:PAD], jnp.float32).astype(jnp.bfloat16)
    table_main = jnp.asarray(combined[PAD:], jnp.float32).astype(jnp.bfloat16)
    return (
        table_hist,
        table_main,
        jnp.asarray(band_taper, jnp.float32),
        jnp.asarray(lag_table, jnp.float32).astype(jnp.bfloat16),
    )


def whiten(spectrum, band_taper):
    amplitude = jnp.sqrt(spectrum[:, 0] * spectrum[:, 0] + spectrum[:, 1] * spectrum[:, 1])
    water_level = 0.5 * (jnp.mean(amplitude, axis=1, keepdims=True) + 1e-05)
    factor = band_taper[None, :, None] / jnp.maximum(amplitude, water_level)
    return (spectrum * factor[:, None]).astype(jnp.bfloat16)


def segment_terms(kept_spec, partner, lag_table):
    rotated = jnp.stack([kept_spec[:, 1], -kept_spec[:, 0]], axis=1)
    stacked_rows = jnp.stack([kept_spec, rotated])
    cross_spec = jnp.einsum(
        "qwpfi,wpfj->fqji", stacked_rows, partner, preferred_element_type=jnp.float32
    ).astype(jnp.bfloat16)
    rows, columns = kept_spec.shape[3], partner.shape[3]
    flat = cross_spec.reshape(2 * F, columns * rows)
    lag_flat = lag_table.transpose(1, 0, 2).reshape(2 * F, LAGS)
    terms = jnp.einsum("kn,kl->ln", flat, lag_flat, preferred_element_type=jnp.float32)
    return terms.astype(jnp.bfloat16).reshape(LAGS, columns, rows)


def ring_reduce(own, position, size, forward, backward):
    half = own.shape[-1] // 2
    halves = []
    for step_sign, route, part in ((-1, forward, own[..., :half]), (1, backward, own[..., half:])):
        chunk = lambda k: lax.dynamic_index_in_dim(part, (position + step_sign * k) % size, 0, keepdims=False)
        partial = chunk(1)
        for k in range(2, size + 1):
            received = route(partial)
            total = received.astype(jnp.float32) + chunk(k % size).astype(jnp.float32)
            partial = total if k == size else total.astype(jnp.bfloat16)
        halves.append(partial)
    return jnp.concatenate(halves, axis=-1)


def tm_route(offset_x, offset_z, size_x, size_z):
    def route(value):
        pairs = []
        for x in range(size_x):
            for z in range(size_z):
                target = ((x + offset_x) % size_x) * size_z + (z + offset_z) % size_z
                pairs.append((x * size_z + z, target))
        return lax.ppermute(value, "tm", pairs)
    return route


def per_device(raw_records, keep_window):
    channels_here = raw_records.shape[0]
    windows_here = keep_window.shape[0]
    segments = lax.axis_size("tm")
    blocks = lax.axis_size("chan")
    table_hist, table_main, band_taper, lag_table = make_tables()
    blocked = raw_records.reshape(channels_here, windows_here, RAWW)
    history = passed_along(raw_records[:, windows_here * RAWW - PAD :], "tm", 1)
    previous = jnp.concatenate([history[:, None, :], blocked[:, :-1, RAWW - PAD :]], axis=1)
    spectrum = jnp.einsum("cwr,rq->wqc", blocked, table_main, preferred_element_type=jnp.float32)
    spectrum = spectrum + jnp.einsum(
        "cwr,rq->wqc", previous, table_hist, preferred_element_type=jnp.float32
    )
    whitened = whiten(spectrum.reshape(windows_here, 2, F, channels_here), band_taper)
    odd = [(b + 1, b) for b in range(0, blocks, 2)]
    partner_near = lax.ppermute(whitened, "chan", [((b + 1) % blocks, b) for b in range(blocks)])
    relayed = lax.ppermute(partner_near, "chan", odd)
    fetched = lax.ppermute(whitened, "chan", [((b + 2) % blocks, b) for b in range(1, blocks, 2)])
    is_odd = lax.axis_index("chan") % 2 == 1
    partner_far = jnp.where(is_odd, fetched, relayed)
    partner = jnp.concatenate([partner_near, partner_far], axis=3)
    kept_spec = whitened * keep_window.astype(jnp.bfloat16)[:, None, None, None]
    terms = segment_terms(kept_spec, partner, lag_table)
    size_z = 4 if segments % 4 == 0 else 1
    size_x = segments // size_z
    row_count = channels_here // segments
    terms = terms.reshape(LAGS, partner.shape[3], size_x, size_z, row_count).transpose(2, 3, 4, 0, 1)
    position = lax.axis_index("tm")
    x_here, z_here = position // size_z, position % size_z
    reduced_x = ring_reduce(
        terms, x_here, size_x, tm_route(1, 0, size_x, size_z), tm_route(-1, 0, size_x, size_z)
    ).astype(jnp.bfloat16)
    reduced = ring_reduce(
        reduced_x, z_here, size_z, tm_route(0, 1, size_x, size_z), tm_route(0, -1, size_x, size_z)
    )
    norm_factor = 1.0 / math.sqrt(windows_here * segments * F)
    return (reduced * norm_factor).astype(jnp.bfloat16)


def solution(mesh):
    placed = (P("chan", "tm"), P("tm"))
    return jax.shard_map(
        per_device,
        mesh=mesh,
        in_specs=placed,
        out_specs=P(("chan", "tm"), None, None),
        check_vma=False,
    )
```

```python
import math

import jax
import jax.numpy as jnp
import numpy as np
from jax import lax
from jax.sharding import Mesh, PartitionSpec as P

W = 256
Q = 5
TAPS = 129
LAGS = 51
F = 128
RAWW = 1280
PAD = 128
TM = ("tx", "tz")


def passed_along(value, axis, by):
    devices = lax.axis_size(axis)
    pairs = [(i, i + by) for i in range(devices) if 0 <= i + by < devices]
    return lax.ppermute(value, axis, pairs)


def shifted(block, axis, distance):
    devices = range(lax.axis_size(axis))
    route = [((i - distance) % len(devices), i) for i in devices]
    return lax.ppermute(block, axis, route)


def make_tables():
    tap_index = np.arange(TAPS)
    centre = (TAPS - 1) / 2.0
    hann_window = 0.5 - 0.5 * np.cos(2.0 * np.pi * (tap_index + 1) / (TAPS + 1))
    sinc_arg = 0.16 * (tap_index - centre)
    safe_arg = np.where(sinc_arg == 0.0, 1.0, sinc_arg)
    sinc_vals = np.where(sinc_arg == 0.0, 1.0, np.sin(np.pi * safe_arg) / (np.pi * safe_arg))
    fir_taps = sinc_vals * hann_window
    fir_taps = fir_taps / fir_taps.sum()
    sample = np.arange(W)
    bin_index = np.arange(F)
    phase_grid = 2.0 * np.pi * np.outer(sample, bin_index) / W
    dft_table = np.concatenate([np.cos(phase_grid), -np.sin(phase_grid)], axis=1)
    combined = np.zeros((PAD + RAWW, 2 * F))
    for tap_number in range(TAPS):
        row_index = Q * sample - tap_number + PAD
        combined[row_index] += fir_taps[tap_number] * dft_table
    rising = np.sin(0.5 * np.pi * np.minimum(1.0, bin_index / 10.0)) ** 2
    falling = np.sin(0.5 * np.pi * np.minimum(1.0, (F - bin_index) / 16.0)) ** 2
    band_taper = rising * falling
    lag_index = np.arange(LAGS) - (LAGS - 1) / 2.0
    lag_phase = 2.0 * np.pi * np.outer(bin_index, lag_index) / W
    weight = np.where(bin_index == 0, 1.0, 2.0)[:, None]
    lag_table = np.stack([weight * np.cos(lag_phase), weight * np.sin(lag_phase)])
    table_hist = jnp.asarray(combined[:PAD], jnp.float32).astype(jnp.bfloat16)
    table_main = jnp.asarray(combined[PAD:], jnp.float32).astype(jnp.bfloat16)
    return (
        table_hist,
        table_main,
        jnp.asarray(band_taper, jnp.float32),
        jnp.asarray(lag_table, jnp.float32).astype(jnp.bfloat16),
    )


def whiten(spectrum, band_taper):
    amplitude = jnp.sqrt(spectrum[:, 0] * spectrum[:, 0] + spectrum[:, 1] * spectrum[:, 1])
    water_level = 0.5 * (jnp.mean(amplitude, axis=1, keepdims=True) + 1e-05)
    factor = band_taper[None, :, None] / jnp.maximum(amplitude, water_level)
    return (spectrum * factor[:, None]).astype(jnp.bfloat16)


def segment_terms(kept_spec, partner, lag_table):
    rotated = jnp.stack([kept_spec[:, 1], -kept_spec[:, 0]], axis=1)
    stacked_rows = jnp.stack([kept_spec, rotated])
    cross_spec = jnp.einsum(
        "qwpfi,wpfj->fqji", stacked_rows, partner, preferred_element_type=jnp.float32
    ).astype(jnp.bfloat16)
    rows, columns = kept_spec.shape[3], partner.shape[3]
    flat = cross_spec.reshape(2 * F, columns * rows)
    lag_flat = lag_table.transpose(1, 0, 2).reshape(2 * F, LAGS)
    terms = jnp.einsum("kn,kl->nl", flat, lag_flat, preferred_element_type=jnp.float32)
    return terms.astype(jnp.bfloat16).reshape(columns, rows, LAGS).transpose(2, 0, 1)


def per_device(raw_records, keep_window):
    channels_here = raw_records.shape[0]
    windows_here = keep_window.shape[0]
    segments = lax.axis_size(TM)
    blocks = lax.axis_size("chan")
    table_hist, table_main, band_taper, lag_table = make_tables()
    blocked = raw_records.reshape(channels_here, windows_here, RAWW)
    history = passed_along(raw_records[:, windows_here * RAWW - PAD :], TM, 1)
    previous = jnp.concatenate([history[:, None, :], blocked[:, :-1, RAWW - PAD :]], axis=1)
    spectrum = jnp.einsum("cwr,rq->wqc", blocked, table_main, preferred_element_type=jnp.float32)
    spectrum = spectrum + jnp.einsum(
        "cwr,rq->wqc", previous, table_hist, preferred_element_type=jnp.float32
    )
    whitened = whiten(spectrum.reshape(windows_here, 2, F, channels_here), band_taper)
    odd = [(b + 1, b) for b in range(0, blocks, 2)]
    partner_near = lax.ppermute(whitened, "chan", [((b + 1) % blocks, b) for b in range(blocks)])
    relayed = lax.ppermute(partner_near, "chan", odd)
    fetched = lax.ppermute(whitened, "chan", [((b + 2) % blocks, b) for b in range(1, blocks, 2)])
    is_odd = lax.axis_index("chan") % 2 == 1
    partner_far = jnp.where(is_odd, fetched, relayed)
    partner = jnp.concatenate([partner_near, partner_far], axis=3)
    kept_spec = whitened * keep_window.astype(jnp.bfloat16)[:, None, None, None]
    terms = segment_terms(kept_spec, partner, lag_table)
    size_x, size_z = lax.axis_size("tx"), lax.axis_size("tz")
    row_count = channels_here // segments
    terms = terms.reshape(LAGS, partner.shape[3], size_x, size_z, row_count).transpose(2, 3, 4, 0, 1)
    over_x = lax.all_to_all(terms, "tx", 0, 0, tiled=True)
    over_x = jnp.sum(over_x.astype(jnp.float32), axis=0).astype(jnp.bfloat16)
    over_z = lax.all_to_all(over_x, "tz", 0, 0, tiled=True)
    reduced = jnp.sum(over_z.astype(jnp.float32), axis=0)
    norm_factor = 1.0 / math.sqrt(windows_here * segments * F)
    return (reduced * norm_factor).astype(jnp.bfloat16)


def solution(mesh):
    chan_size, tm_size = mesh.devices.shape
    split_z = 4 if tm_size % 4 == 0 else 1
    grid = Mesh(mesh.devices.reshape(chan_size, tm_size // split_z, split_z), ("chan",) + TM)
    placed = (P("chan", TM), P(TM))
    return jax.shard_map(
        per_device,
        mesh=grid,
        in_specs=placed,
        out_specs=P(("chan",) + TM, None, None),
        check_vma=False,
    )
```

```python
import math

import jax
import jax.numpy as jnp
import numpy as np
from jax import lax
from jax.sharding import Mesh, PartitionSpec as P

W = 256
Q = 5
TAPS = 129
LAGS = 51
F = 128
RAWW = 1280
PAD = 128
TM = ("tx", "tz")


def passed_along(value, axis, by):
    devices = lax.axis_size(axis)
    pairs = [(i, i + by) for i in range(devices) if 0 <= i + by < devices]
    return lax.ppermute(value, axis, pairs)


def shifted(block, axis, distance):
    devices = range(lax.axis_size(axis))
    route = [((i - distance) % len(devices), i) for i in devices]
    return lax.ppermute(block, axis, route)


def make_tables():
    tap_index = np.arange(TAPS)
    centre = (TAPS - 1) / 2.0
    hann_window = 0.5 - 0.5 * np.cos(2.0 * np.pi * (tap_index + 1) / (TAPS + 1))
    sinc_arg = 0.16 * (tap_index - centre)
    safe_arg = np.where(sinc_arg == 0.0, 1.0, sinc_arg)
    sinc_vals = np.where(sinc_arg == 0.0, 1.0, np.sin(np.pi * safe_arg) / (np.pi * safe_arg))
    fir_taps = sinc_vals * hann_window
    fir_taps = fir_taps / fir_taps.sum()
    sample = np.arange(W)
    bin_index = np.arange(F)
    phase_grid = 2.0 * np.pi * np.outer(sample, bin_index) / W
    dft_table = np.concatenate([np.cos(phase_grid), -np.sin(phase_grid)], axis=1)
    combined = np.zeros((PAD + RAWW, 2 * F))
    for tap_number in range(TAPS):
        row_index = Q * sample - tap_number + PAD
        combined[row_index] += fir_taps[tap_number] * dft_table
    rising = np.sin(0.5 * np.pi * np.minimum(1.0, bin_index / 10.0)) ** 2
    falling = np.sin(0.5 * np.pi * np.minimum(1.0, (F - bin_index) / 16.0)) ** 2
    band_taper = rising * falling
    lag_index = np.arange(LAGS) - (LAGS - 1) / 2.0
    lag_phase = 2.0 * np.pi * np.outer(bin_index, lag_index) / W
    weight = np.where(bin_index == 0, 1.0, 2.0)[:, None]
    lag_table = np.stack([weight * np.cos(lag_phase), weight * np.sin(lag_phase)])
    table_hist = jnp.asarray(combined[:PAD], jnp.float32).astype(jnp.bfloat16)
    table_main = jnp.asarray(combined[PAD:], jnp.float32).astype(jnp.bfloat16)
    return (
        table_hist,
        table_main,
        jnp.asarray(band_taper, jnp.float32),
        jnp.asarray(lag_table, jnp.float32).astype(jnp.bfloat16),
    )


def whiten(spectrum, band_taper):
    amplitude = jnp.sqrt(spectrum[:, 0] * spectrum[:, 0] + spectrum[:, 1] * spectrum[:, 1])
    water_level = 0.5 * (jnp.mean(amplitude, axis=1, keepdims=True) + 1e-05)
    factor = band_taper[None, :, None] / jnp.maximum(amplitude, water_level)
    return (spectrum * factor[:, None]).astype(jnp.bfloat16)


def segment_terms(kept_spec, partner, lag_table):
    rotated = jnp.stack([kept_spec[:, 1], -kept_spec[:, 0]], axis=1)
    stacked_rows = jnp.stack([kept_spec, rotated])
    cross_spec = jnp.einsum(
        "qwpfi,wpfj->fqji", stacked_rows, partner, preferred_element_type=jnp.float32
    ).astype(jnp.bfloat16)
    bins, rows, columns = kept_spec.shape[2], kept_spec.shape[3], partner.shape[3]
    flat = cross_spec.reshape(2 * bins, columns * rows)
    lag_flat = lag_table.transpose(1, 0, 2).reshape(2 * bins, LAGS)
    return jnp.einsum("kn,kl->nl", flat, lag_flat, preferred_element_type=jnp.float32)


def partners(whitened, blocks):
    odd = [(b + 1, b) for b in range(0, blocks, 2)]
    partner_near = lax.ppermute(whitened, "chan", [((b + 1) % blocks, b) for b in range(blocks)])
    fetched = lax.ppermute(whitened, "chan", [((b + 2) % blocks, b) for b in range(1, blocks, 2)])
    return partner_near, fetched, odd


def per_device(raw_records, keep_window):
    channels_here = raw_records.shape[0]
    windows_here = keep_window.shape[0]
    segments = lax.axis_size(TM)
    blocks = lax.axis_size("chan")
    table_hist, table_main, band_taper, lag_table = make_tables()
    blocked = raw_records.reshape(channels_here, windows_here, RAWW)
    history = passed_along(raw_records[:, windows_here * RAWW - PAD :], TM, 1)
    previous = jnp.concatenate([history[:, None, :], blocked[:, :-1, RAWW - PAD :]], axis=1)
    spectrum = jnp.einsum("cwr,rq->wqc", blocked, table_main, preferred_element_type=jnp.float32)
    spectrum = spectrum + jnp.einsum(
        "cwr,rq->wqc", previous, table_hist, preferred_element_type=jnp.float32
    )
    whitened = whiten(spectrum.reshape(windows_here, 2, F, channels_here), band_taper)
    kept_spec = whitened * keep_window.astype(jnp.bfloat16)[:, None, None, None]
    is_odd = lax.axis_index("chan") % 2 == 1
    split = F // 2
    pending = whitened[:, :, split:]
    terms = None
    for first_bin, last_bin in ((0, split), (split, F)):
        sent = whitened[:, :, :split] if first_bin == 0 else pending
        partner_near, fetched, odd = partners(sent, blocks)
        if first_bin == 0:
            partner_near, fetched, pending = lax.optimization_barrier((partner_near, fetched, pending))
        relayed = lax.ppermute(partner_near, "chan", odd)
        partner = jnp.concatenate([partner_near, jnp.where(is_odd, fetched, relayed)], axis=3)
        part = segment_terms(kept_spec[:, :, first_bin:last_bin], partner, lag_table[:, first_bin:last_bin])
        terms = part if terms is None else terms + part
    columns = 2 * channels_here
    terms = terms.astype(jnp.bfloat16).reshape(columns, channels_here, LAGS).transpose(2, 0, 1)
    size_x, size_z = lax.axis_size("tx"), lax.axis_size("tz")
    row_count = channels_here // segments
    terms = terms.reshape(LAGS, columns, size_x, size_z, row_count).transpose(2, 3, 4, 0, 1)
    over_x = lax.all_to_all(terms, "tx", 0, 0, tiled=True)
    over_x = jnp.sum(over_x.astype(jnp.float32), axis=0).astype(jnp.bfloat16)
    over_z = lax.all_to_all(over_x, "tz", 0, 0, tiled=True)
    reduced = jnp.sum(over_z.astype(jnp.float32), axis=0)
    norm_factor = 1.0 / math.sqrt(windows_here * segments * F)
    return (reduced * norm_factor).astype(jnp.bfloat16)


def solution(mesh):
    chan_size, tm_size = mesh.devices.shape
    split_z = 4 if tm_size % 4 == 0 else 1
    grid = Mesh(mesh.devices.reshape(chan_size, tm_size // split_z, split_z), ("chan",) + TM)
    placed = (P("chan", TM), P(TM))
    return jax.shard_map(
        per_device,
        mesh=grid,
        in_specs=placed,
        out_specs=P(("chan",) + TM, None, None),
        check_vma=False,
    )
```

```python
import math

import jax
import jax.numpy as jnp
import numpy as np
from jax import lax
from jax.sharding import Mesh, PartitionSpec as P

W = 256
Q = 5
TAPS = 129
LAGS = 51
F = 128
RAWW = 1280
PAD = 128
TM = ("tx", "tz")


def passed_along(value, axis, by):
    devices = lax.axis_size(axis)
    pairs = [(i, i + by) for i in range(devices) if 0 <= i + by < devices]
    return lax.ppermute(value, axis, pairs)


def shifted(block, axis, distance):
    devices = range(lax.axis_size(axis))
    route = [((i - distance) % len(devices), i) for i in devices]
    return lax.ppermute(block, axis, route)


def make_tables():
    tap_index = np.arange(TAPS)
    centre = (TAPS - 1) / 2.0
    hann_window = 0.5 - 0.5 * np.cos(2.0 * np.pi * (tap_index + 1) / (TAPS + 1))
    sinc_arg = 0.16 * (tap_index - centre)
    safe_arg = np.where(sinc_arg == 0.0, 1.0, sinc_arg)
    sinc_vals = np.where(sinc_arg == 0.0, 1.0, np.sin(np.pi * safe_arg) / (np.pi * safe_arg))
    fir_taps = sinc_vals * hann_window
    fir_taps = fir_taps / fir_taps.sum()
    sample = np.arange(W)
    bin_index = np.arange(F)
    phase_grid = 2.0 * np.pi * np.outer(sample, bin_index) / W
    dft_table = np.concatenate([np.cos(phase_grid), -np.sin(phase_grid)], axis=1)
    combined = np.zeros((PAD + RAWW, 2 * F))
    for tap_number in range(TAPS):
        row_index = Q * sample - tap_number + PAD
        combined[row_index] += fir_taps[tap_number] * dft_table
    rising = np.sin(0.5 * np.pi * np.minimum(1.0, bin_index / 10.0)) ** 2
    falling = np.sin(0.5 * np.pi * np.minimum(1.0, (F - bin_index) / 16.0)) ** 2
    band_taper = rising * falling
    lag_index = np.arange(LAGS) - (LAGS - 1) / 2.0
    lag_phase = 2.0 * np.pi * np.outer(bin_index, lag_index) / W
    weight = np.where(bin_index == 0, 1.0, 2.0)[:, None]
    lag_table = np.stack([weight * np.cos(lag_phase), weight * np.sin(lag_phase)])
    table_hist = jnp.asarray(combined[:PAD], jnp.float32).astype(jnp.bfloat16)
    table_main = jnp.asarray(combined[PAD:], jnp.float32).astype(jnp.bfloat16)
    return (
        table_hist,
        table_main,
        jnp.asarray(band_taper, jnp.float32),
        jnp.asarray(lag_table, jnp.float32).astype(jnp.bfloat16),
    )


def whiten(spectrum, band_taper):
    amplitude = jnp.sqrt(spectrum[:, 0] * spectrum[:, 0] + spectrum[:, 1] * spectrum[:, 1])
    water_level = 0.5 * (jnp.mean(amplitude, axis=1, keepdims=True) + 1e-05)
    factor = band_taper[None, :, None] / jnp.maximum(amplitude, water_level)
    return (spectrum * factor[:, None]).astype(jnp.bfloat16)


def segment_terms(stacked_rows, partner, lag_table):
    cross_spec = jnp.einsum(
        "qwpfi,wpfj->fqji", stacked_rows, partner, preferred_element_type=jnp.float32
    ).astype(jnp.bfloat16)
    rows, columns = stacked_rows.shape[4], partner.shape[3]
    flat = cross_spec.reshape(2 * F, columns * rows)
    lag_flat = lag_table.transpose(1, 0, 2).reshape(2 * F, LAGS)
    terms = jnp.einsum("kn,kl->nl", flat, lag_flat, preferred_element_type=jnp.float32)
    return terms.astype(jnp.bfloat16).reshape(columns, rows, LAGS)


def per_device(raw_records, keep_window):
    channels_here = raw_records.shape[0]
    windows_here = keep_window.shape[0]
    segments = lax.axis_size(TM)
    blocks = lax.axis_size("chan")
    table_hist, table_main, band_taper, lag_table = make_tables()
    blocked = raw_records.reshape(channels_here, windows_here, RAWW)
    history = passed_along(raw_records[:, windows_here * RAWW - PAD :], TM, 1)
    previous = jnp.concatenate([history[:, None, :], blocked[:, :-1, RAWW - PAD :]], axis=1)
    spectrum = jnp.einsum("cwr,rq->wqc", blocked, table_main, preferred_element_type=jnp.float32)
    spectrum = spectrum + jnp.einsum(
        "cwr,rq->wqc", previous, table_hist, preferred_element_type=jnp.float32
    )
    whitened = whiten(spectrum.reshape(windows_here, 2, F, channels_here), band_taper)
    odd = [(b + 1, b) for b in range(0, blocks, 2)]
    partner_near = lax.ppermute(whitened, "chan", [((b + 1) % blocks, b) for b in range(blocks)])
    relayed = lax.ppermute(partner_near, "chan", odd)
    fetched = lax.ppermute(whitened, "chan", [((b + 2) % blocks, b) for b in range(1, blocks, 2)])
    is_odd = lax.axis_index("chan") % 2 == 1
    partner_far = jnp.where(is_odd, fetched, relayed)
    kept_spec = whitened * keep_window.astype(jnp.bfloat16)[:, None, None, None]
    rotated = jnp.stack([kept_spec[:, 1], -kept_spec[:, 0]], axis=1)
    stacked_rows = jnp.stack([kept_spec, rotated])
    terms = jnp.concatenate(
        [segment_terms(stacked_rows, partner, lag_table) for partner in (partner_near, partner_far)],
        axis=0,
    ).transpose(2, 0, 1)
    columns = terms.shape[1]
    size_x, size_z = lax.axis_size("tx"), lax.axis_size("tz")
    row_count = channels_here // segments
    terms = terms.reshape(LAGS, columns, size_x, size_z, row_count).transpose(2, 3, 4, 0, 1)
    over_x = lax.all_to_all(terms, "tx", 0, 0, tiled=True)
    over_x = jnp.sum(over_x.astype(jnp.float32), axis=0).astype(jnp.bfloat16)
    over_z = lax.all_to_all(over_x, "tz", 0, 0, tiled=True)
    reduced = jnp.sum(over_z.astype(jnp.float32), axis=0)
    norm_factor = 1.0 / math.sqrt(windows_here * segments * F)
    return (reduced * norm_factor).astype(jnp.bfloat16)


def solution(mesh):
    chan_size, tm_size = mesh.devices.shape
    split_z = 4 if tm_size % 4 == 0 else 1
    grid = Mesh(mesh.devices.reshape(chan_size, tm_size // split_z, split_z), ("chan",) + TM)
    placed = (P("chan", TM), P(TM))
    return jax.shard_map(
        per_device,
        mesh=grid,
        in_specs=placed,
        out_specs=P(("chan",) + TM, None, None),
        check_vma=False,
    )
```

```python
import math

import jax
import jax.numpy as jnp
import numpy as np
from jax import lax
from jax.sharding import Mesh, PartitionSpec as P

W = 256
Q = 5
TAPS = 129
LAGS = 51
F = 128
RAWW = 1280
PAD = 128
TM = ("tx", "tz")


def passed_along(value, axis, by):
    devices = lax.axis_size(axis)
    pairs = [(i, i + by) for i in range(devices) if 0 <= i + by < devices]
    return lax.ppermute(value, axis, pairs)


def shifted(block, axis, distance):
    devices = range(lax.axis_size(axis))
    route = [((i - distance) % len(devices), i) for i in devices]
    return lax.ppermute(block, axis, route)


def make_tables():
    tap_index = np.arange(TAPS)
    centre = (TAPS - 1) / 2.0
    hann_window = 0.5 - 0.5 * np.cos(2.0 * np.pi * (tap_index + 1) / (TAPS + 1))
    sinc_arg = 0.16 * (tap_index - centre)
    safe_arg = np.where(sinc_arg == 0.0, 1.0, sinc_arg)
    sinc_vals = np.where(sinc_arg == 0.0, 1.0, np.sin(np.pi * safe_arg) / (np.pi * safe_arg))
    fir_taps = sinc_vals * hann_window
    fir_taps = fir_taps / fir_taps.sum()
    sample = np.arange(W)
    bin_index = np.arange(F)
    phase_grid = 2.0 * np.pi * np.outer(sample, bin_index) / W
    dft_table = np.concatenate([np.cos(phase_grid), -np.sin(phase_grid)], axis=1)
    combined = np.zeros((PAD + RAWW, 2 * F))
    for tap_number in range(TAPS):
        row_index = Q * sample - tap_number + PAD
        combined[row_index] += fir_taps[tap_number] * dft_table
    rising = np.sin(0.5 * np.pi * np.minimum(1.0, bin_index / 10.0)) ** 2
    falling = np.sin(0.5 * np.pi * np.minimum(1.0, (F - bin_index) / 16.0)) ** 2
    band_taper = rising * falling
    lag_index = np.arange(LAGS) - (LAGS - 1) / 2.0
    lag_phase = 2.0 * np.pi * np.outer(bin_index, lag_index) / W
    weight = np.where(bin_index == 0, 1.0, 2.0)[:, None]
    lag_table = np.stack([weight * np.cos(lag_phase), weight * np.sin(lag_phase)])
    table_hist = jnp.asarray(combined[:PAD], jnp.float32).astype(jnp.bfloat16)
    table_main = jnp.asarray(combined[PAD:], jnp.float32).astype(jnp.bfloat16)
    return (
        table_hist,
        table_main,
        jnp.asarray(band_taper, jnp.float32),
        jnp.asarray(lag_table, jnp.float32).astype(jnp.bfloat16),
    )


def whiten(spectrum, band_taper):
    amplitude = jnp.sqrt(spectrum[:, 0] * spectrum[:, 0] + spectrum[:, 1] * spectrum[:, 1])
    water_level = 0.5 * (jnp.mean(amplitude, axis=1, keepdims=True) + 1e-05)
    factor = band_taper[None, :, None] / jnp.maximum(amplitude, water_level)
    return (spectrum * factor[:, None]).astype(jnp.bfloat16)


def segment_terms(stacked_rows, partner, lag_table):
    cross_spec = jnp.einsum(
        "qwpfi,wpfj->fqji", stacked_rows, partner, preferred_element_type=jnp.float32
    ).astype(jnp.bfloat16)
    rows, columns = stacked_rows.shape[4], partner.shape[3]
    flat = cross_spec.reshape(2 * F, columns * rows)
    lag_flat = lag_table.transpose(1, 0, 2).reshape(2 * F, LAGS)
    terms = jnp.einsum("kn,kl->nl", flat, lag_flat, preferred_element_type=jnp.float32)
    return terms.astype(jnp.bfloat16).reshape(columns, rows, LAGS)


def per_device(raw_records, keep_window):
    channels_here = raw_records.shape[0]
    windows_here = keep_window.shape[0]
    segments = lax.axis_size(TM)
    blocks = lax.axis_size("chan")
    table_hist, table_main, band_taper, lag_table = make_tables()
    blocked = raw_records.reshape(channels_here, windows_here, RAWW)
    history = passed_along(raw_records[:, windows_here * RAWW - PAD :], TM, 1)
    previous = jnp.concatenate([history[:, None, :], blocked[:, :-1, RAWW - PAD :]], axis=1)
    spectrum = jnp.einsum("cwr,rq->wqc", blocked, table_main, preferred_element_type=jnp.float32)
    spectrum = spectrum + jnp.einsum(
        "cwr,rq->wqc", previous, table_hist, preferred_element_type=jnp.float32
    )
    whitened = whiten(spectrum.reshape(windows_here, 2, F, channels_here), band_taper)
    odd = [(b + 1, b) for b in range(0, blocks, 2)]
    partner_near = lax.ppermute(whitened, "chan", [((b + 1) % blocks, b) for b in range(blocks)])
    relayed = lax.ppermute(partner_near, "chan", odd)
    fetched = lax.ppermute(whitened, "chan", [((b + 2) % blocks, b) for b in range(1, blocks, 2)])
    is_odd = lax.axis_index("chan") % 2 == 1
    partner_far = jnp.where(is_odd, fetched, relayed)
    kept_spec = whitened * keep_window.astype(jnp.bfloat16)[:, None, None, None]
    rotated = jnp.stack([kept_spec[:, 1], -kept_spec[:, 0]], axis=1)
    stacked_rows = jnp.stack([kept_spec, rotated])
    size_x, size_z = lax.axis_size("tx"), lax.axis_size("tz")
    row_count = channels_here // segments
    sums = []
    for partner in (partner_near, partner_far):
        terms = segment_terms(stacked_rows, partner, lag_table)
        columns = terms.shape[0]
        terms = terms.reshape(columns, size_x, size_z, row_count, LAGS).transpose(1, 2, 3, 4, 0)
        over_x = lax.all_to_all(terms, "tx", 0, 0, tiled=True)
        over_x = jnp.sum(over_x.astype(jnp.float32), axis=0).astype(jnp.bfloat16)
        over_z = lax.all_to_all(over_x, "tz", 0, 0, tiled=True)
        sums.append(jnp.sum(over_z.astype(jnp.float32), axis=0))
    reduced = jnp.concatenate(sums, axis=2)
    norm_factor = 1.0 / math.sqrt(windows_here * segments * F)
    return (reduced * norm_factor).astype(jnp.bfloat16)


def solution(mesh):
    chan_size, tm_size = mesh.devices.shape
    split_z = 4 if tm_size % 4 == 0 else 1
    grid = Mesh(mesh.devices.reshape(chan_size, tm_size // split_z, split_z), ("chan",) + TM)
    placed = (P("chan", TM), P(TM))
    return jax.shard_map(
        per_device,
        mesh=grid,
        in_specs=placed,
        out_specs=P(("chan",) + TM, None, None),
        check_vma=False,
    )
```

```python
import math

import jax
import jax.numpy as jnp
import numpy as np
from jax import lax
from jax.sharding import Mesh, PartitionSpec as P

W = 256
Q = 5
TAPS = 129
LAGS = 51
F = 128
RAWW = 1280
PAD = 128
TM = ("tx", "tz")


def passed_along(value, axis, by):
    devices = lax.axis_size(axis)
    pairs = [(i, i + by) for i in range(devices) if 0 <= i + by < devices]
    return lax.ppermute(value, axis, pairs)


def shifted(block, axis, distance):
    devices = range(lax.axis_size(axis))
    route = [((i - distance) % len(devices), i) for i in devices]
    return lax.ppermute(block, axis, route)


def make_tables():
    tap_index = np.arange(TAPS)
    centre = (TAPS - 1) / 2.0
    hann_window = 0.5 - 0.5 * np.cos(2.0 * np.pi * (tap_index + 1) / (TAPS + 1))
    sinc_arg = 0.16 * (tap_index - centre)
    safe_arg = np.where(sinc_arg == 0.0, 1.0, sinc_arg)
    sinc_vals = np.where(sinc_arg == 0.0, 1.0, np.sin(np.pi * safe_arg) / (np.pi * safe_arg))
    fir_taps = sinc_vals * hann_window
    fir_taps = fir_taps / fir_taps.sum()
    sample = np.arange(W)
    bin_index = np.arange(F)
    phase_grid = 2.0 * np.pi * np.outer(sample, bin_index) / W
    dft_table = np.concatenate([np.cos(phase_grid), -np.sin(phase_grid)], axis=1)
    combined = np.zeros((PAD + RAWW, 2 * F))
    for tap_number in range(TAPS):
        row_index = Q * sample - tap_number + PAD
        combined[row_index] += fir_taps[tap_number] * dft_table
    rising = np.sin(0.5 * np.pi * np.minimum(1.0, bin_index / 10.0)) ** 2
    falling = np.sin(0.5 * np.pi * np.minimum(1.0, (F - bin_index) / 16.0)) ** 2
    band_taper = rising * falling
    lag_index = np.arange(LAGS) - (LAGS - 1) / 2.0
    lag_phase = 2.0 * np.pi * np.outer(bin_index, lag_index) / W
    weight = np.where(bin_index == 0, 1.0, 2.0)[:, None]
    lag_table = np.stack([weight * np.cos(lag_phase), weight * np.sin(lag_phase)])
    table_hist = jnp.asarray(combined[:PAD], jnp.float32).astype(jnp.bfloat16)
    table_main = jnp.asarray(combined[PAD:], jnp.float32).astype(jnp.bfloat16)
    return (
        table_hist,
        table_main,
        jnp.asarray(band_taper, jnp.float32),
        jnp.asarray(lag_table, jnp.float32).astype(jnp.bfloat16),
    )


def whiten(spectrum, band_taper):
    amplitude = jnp.sqrt(spectrum[:, 0] * spectrum[:, 0] + spectrum[:, 1] * spectrum[:, 1])
    water_level = 0.5 * (jnp.mean(amplitude, axis=1, keepdims=True) + 1e-05)
    factor = band_taper[None, :, None] / jnp.maximum(amplitude, water_level)
    return (spectrum * factor[:, None]).astype(jnp.bfloat16)


def segment_terms(stacked_rows, partner, lag_table):
    cross_spec = jnp.einsum(
        "qwpfi,wpfj->fqji", stacked_rows, partner, preferred_element_type=jnp.float32
    ).astype(jnp.bfloat16)
    rows, columns = stacked_rows.shape[4], partner.shape[3]
    flat = cross_spec.reshape(2 * F, columns * rows)
    lag_flat = lag_table.transpose(1, 0, 2).reshape(2 * F, LAGS)
    terms = jnp.einsum("kn,kl->nl", flat, lag_flat, preferred_element_type=jnp.float32)
    return terms.astype(jnp.bfloat16).reshape(columns, rows, LAGS)


def per_device(raw_records, keep_window):
    channels_here = raw_records.shape[0]
    windows_here = keep_window.shape[0]
    segments = lax.axis_size(TM)
    blocks = lax.axis_size("chan")
    table_hist, table_main, band_taper, lag_table = make_tables()
    blocked = raw_records.reshape(channels_here, windows_here, RAWW)
    history = passed_along(raw_records[:, windows_here * RAWW - PAD :], TM, 1)
    previous = jnp.concatenate([history[:, None, :], blocked[:, :-1, RAWW - PAD :]], axis=1)
    spectrum = jnp.einsum("cwr,rq->wqc", blocked, table_main, preferred_element_type=jnp.float32)
    spectrum = spectrum + jnp.einsum(
        "cwr,rq->wqc", previous, table_hist, preferred_element_type=jnp.float32
    )
    whitened = whiten(spectrum.reshape(windows_here, 2, F, channels_here), band_taper)
    odd = [(b + 1, b) for b in range(0, blocks, 2)]
    partner_near = lax.ppermute(whitened, "chan", [((b + 1) % blocks, b) for b in range(blocks)])
    relayed = lax.ppermute(partner_near, "chan", odd)
    fetched = lax.ppermute(whitened, "chan", [((b + 2) % blocks, b) for b in range(1, blocks, 2)])
    is_odd = lax.axis_index("chan") % 2 == 1
    partner_far = jnp.where(is_odd, fetched, relayed)
    kept_spec = whitened * keep_window.astype(jnp.bfloat16)[:, None, None, None]
    rotated = jnp.stack([kept_spec[:, 1], -kept_spec[:, 0]], axis=1)
    stacked_rows = jnp.stack([kept_spec, rotated])
    terms = jnp.concatenate(
        [segment_terms(stacked_rows, partner, lag_table) for partner in (partner_near, partner_far)],
        axis=0,
    ).transpose(2, 0, 1)
    columns = terms.shape[1]
    size_x, size_z = lax.axis_size("tx"), lax.axis_size("tz")
    row_count = channels_here // segments
    terms = terms.reshape(LAGS, columns, size_x, size_z, row_count).transpose(2, 3, 4, 0, 1)
    split = (LAGS * 3) // 7
    offload = terms[:, :, :, :split].reshape(channels_here, split * columns)
    offload = lax.psum_scatter(offload, TM, scatter_dimension=0, tiled=True)
    over_x = lax.all_to_all(terms[:, :, :, split:], "tx", 0, 0, tiled=True)
    over_x = jnp.sum(over_x.astype(jnp.float32), axis=0).astype(jnp.bfloat16)
    over_z = lax.all_to_all(over_x, "tz", 0, 0, tiled=True)
    reduced = jnp.concatenate(
        [offload.reshape(row_count, split, columns).astype(jnp.float32), jnp.sum(over_z.astype(jnp.float32), axis=0)],
        axis=1,
    )
    norm_factor = 1.0 / math.sqrt(windows_here * segments * F)
    return (reduced * norm_factor).astype(jnp.bfloat16)


def solution(mesh):
    chan_size, tm_size = mesh.devices.shape
    split_z = 4 if tm_size % 4 == 0 else 1
    grid = Mesh(mesh.devices.reshape(chan_size, tm_size // split_z, split_z), ("chan",) + TM)
    placed = (P("chan", TM), P(TM))
    return jax.shard_map(
        per_device,
        mesh=grid,
        in_specs=placed,
        out_specs=P(("chan",) + TM, None, None),
        check_vma=False,
    )
```

```python
import math

import jax
import jax.numpy as jnp
import numpy as np
from jax import lax
from jax.sharding import Mesh, PartitionSpec as P

W = 256
Q = 5
TAPS = 129
LAGS = 51
F = 128
RAWW = 1280
PAD = 128
TM = ("tx", "tz")


def passed_along(value, axis, by):
    devices = lax.axis_size(axis)
    pairs = [(i, i + by) for i in range(devices) if 0 <= i + by < devices]
    return lax.ppermute(value, axis, pairs)


def shifted(block, axis, distance):
    devices = range(lax.axis_size(axis))
    route = [((i - distance) % len(devices), i) for i in devices]
    return lax.ppermute(block, axis, route)


def make_tables():
    tap_index = np.arange(TAPS)
    centre = (TAPS - 1) / 2.0
    hann_window = 0.5 - 0.5 * np.cos(2.0 * np.pi * (tap_index + 1) / (TAPS + 1))
    sinc_arg = 0.16 * (tap_index - centre)
    safe_arg = np.where(sinc_arg == 0.0, 1.0, sinc_arg)
    sinc_vals = np.where(sinc_arg == 0.0, 1.0, np.sin(np.pi * safe_arg) / (np.pi * safe_arg))
    fir_taps = sinc_vals * hann_window
    fir_taps = fir_taps / fir_taps.sum()
    sample = np.arange(W)
    bin_index = np.arange(F)
    phase_grid = 2.0 * np.pi * np.outer(sample, bin_index) / W
    dft_table = np.concatenate([np.cos(phase_grid), -np.sin(phase_grid)], axis=1)
    combined = np.zeros((PAD + RAWW, 2 * F))
    for tap_number in range(TAPS):
        row_index = Q * sample - tap_number + PAD
        combined[row_index] += fir_taps[tap_number] * dft_table
    rising = np.sin(0.5 * np.pi * np.minimum(1.0, bin_index / 10.0)) ** 2
    falling = np.sin(0.5 * np.pi * np.minimum(1.0, (F - bin_index) / 16.0)) ** 2
    band_taper = rising * falling
    lag_index = np.arange(LAGS) - (LAGS - 1) / 2.0
    lag_phase = 2.0 * np.pi * np.outer(bin_index, lag_index) / W
    weight = np.where(bin_index == 0, 1.0, 2.0)[:, None]
    lag_table = np.stack([weight * np.cos(lag_phase), weight * np.sin(lag_phase)])
    table_hist = jnp.asarray(combined[:PAD], jnp.float32).astype(jnp.bfloat16)
    table_main = jnp.asarray(combined[PAD:], jnp.float32).astype(jnp.bfloat16)
    return (
        table_hist,
        table_main,
        jnp.asarray(band_taper, jnp.float32),
        jnp.asarray(lag_table, jnp.float32).astype(jnp.bfloat16),
    )


def whiten(spectrum, band_taper):
    amplitude = jnp.sqrt(spectrum[:, 0] * spectrum[:, 0] + spectrum[:, 1] * spectrum[:, 1])
    water_level = 0.5 * (jnp.mean(amplitude, axis=1, keepdims=True) + 1e-05)
    factor = band_taper[None, :, None] / jnp.maximum(amplitude, water_level)
    return (spectrum * factor[:, None]).astype(jnp.bfloat16)


def segment_terms(stacked_rows, partner, lag_table):
    cross_spec = jnp.einsum(
        "qwpfi,wpfj->fqji", stacked_rows, partner, preferred_element_type=jnp.float32
    ).astype(jnp.bfloat16)
    rows, columns = stacked_rows.shape[4], partner.shape[3]
    flat = cross_spec.reshape(2 * F, columns * rows)
    lag_flat = lag_table.transpose(1, 0, 2).reshape(2 * F, LAGS)
    terms = jnp.einsum("kn,kl->nl", flat, lag_flat, preferred_element_type=jnp.float32)
    return terms.astype(jnp.bfloat16).reshape(columns, rows, LAGS)


def relay_routes(blocks, segments):
    def device(block, segment):
        return block * segments + segment

    def place(z, y, core, x):
        z %= 8
        return device((y * 2 + z // 4) * 2 + core, x * 4 + z % 4)

    hop, near_route, far_route = [], [], []
    for target in range(1, blocks, 2):
        for segment in range(segments):
            x, z_lo = segment // 4, segment % 4
            for step, route in ((1, near_route), (2, far_route)):
                source = (target + step) % blocks
                y, z_hi, core = source // 4, (source // 2) % 2, source % 2
                z = z_hi * 4 + z_lo
                turn = -1 if core == 0 else 1
                relay = place(z + turn, y, core, x)
                hop.append((device(source, segment), relay))
                route.append((relay, device(target, segment)))
    return hop, near_route, far_route


def per_device(raw_records, keep_window):
    channels_here = raw_records.shape[0]
    windows_here = keep_window.shape[0]
    segments = lax.axis_size(TM)
    blocks = lax.axis_size("chan")
    table_hist, table_main, band_taper, lag_table = make_tables()
    blocked = raw_records.reshape(channels_here, windows_here, RAWW)
    history = passed_along(raw_records[:, windows_here * RAWW - PAD :], TM, 1)
    previous = jnp.concatenate([history[:, None, :], blocked[:, :-1, RAWW - PAD :]], axis=1)
    spectrum = jnp.einsum("cwr,rq->wqc", blocked, table_main, preferred_element_type=jnp.float32)
    spectrum = spectrum + jnp.einsum(
        "cwr,rq->wqc", previous, table_hist, preferred_element_type=jnp.float32
    )
    whitened = whiten(spectrum.reshape(windows_here, 2, F, channels_here), band_taper)
    hop, near_route, far_route = relay_routes(blocks, segments)
    every = ("chan",) + TM
    passed = lax.ppermute(whitened, every, hop)
    is_odd = lax.axis_index("chan") % 2 == 1
    arrived_near = lax.ppermute(passed, every, near_route)
    arrived_far = lax.ppermute(passed, every, far_route)
    beside = [(b + 1, b) for b in range(0, blocks, 2)]
    own_near = lax.ppermute(whitened, "chan", beside)
    partner_near = jnp.where(is_odd, arrived_near, own_near)
    partner_far = jnp.where(is_odd, arrived_far, lax.ppermute(arrived_near, "chan", beside))
    kept_spec = whitened * keep_window.astype(jnp.bfloat16)[:, None, None, None]
    rotated = jnp.stack([kept_spec[:, 1], -kept_spec[:, 0]], axis=1)
    stacked_rows = jnp.stack([kept_spec, rotated])
    terms = jnp.concatenate(
        [segment_terms(stacked_rows, partner, lag_table) for partner in (partner_near, partner_far)],
        axis=0,
    ).transpose(2, 0, 1)
    columns = terms.shape[1]
    size_x, size_z = lax.axis_size("tx"), lax.axis_size("tz")
    row_count = channels_here // segments
    terms = terms.reshape(LAGS, columns, size_x, size_z, row_count).transpose(2, 3, 4, 0, 1)
    over_x = lax.all_to_all(terms, "tx", 0, 0, tiled=True)
    over_x = jnp.sum(over_x.astype(jnp.float32), axis=0).astype(jnp.bfloat16)
    over_z = lax.all_to_all(over_x, "tz", 0, 0, tiled=True)
    reduced = jnp.sum(over_z.astype(jnp.float32), axis=0)
    norm_factor = 1.0 / math.sqrt(windows_here * segments * F)
    return (reduced * norm_factor).astype(jnp.bfloat16)


def solution(mesh):
    chan_size, tm_size = mesh.devices.shape
    split_z = 4 if tm_size % 4 == 0 else 1
    grid = Mesh(mesh.devices.reshape(chan_size, tm_size // split_z, split_z), ("chan",) + TM)
    placed = (P("chan", TM), P(TM))
    return jax.shard_map(
        per_device,
        mesh=grid,
        in_specs=placed,
        out_specs=P(("chan",) + TM, None, None),
        check_vma=False,
    )
```

```python
import math

import jax
import jax.numpy as jnp
import numpy as np
from jax import lax
from jax.sharding import Mesh, PartitionSpec as P

W = 256
Q = 5
TAPS = 129
LAGS = 51
F = 128
RAWW = 1280
PAD = 128
TM = ("tx", "tz")


def passed_along(value, axis, by):
    devices = lax.axis_size(axis)
    pairs = [(i, i + by) for i in range(devices) if 0 <= i + by < devices]
    return lax.ppermute(value, axis, pairs)


def shifted(block, axis, distance):
    devices = range(lax.axis_size(axis))
    route = [((i - distance) % len(devices), i) for i in devices]
    return lax.ppermute(block, axis, route)


def make_tables():
    tap_index = np.arange(TAPS)
    centre = (TAPS - 1) / 2.0
    hann_window = 0.5 - 0.5 * np.cos(2.0 * np.pi * (tap_index + 1) / (TAPS + 1))
    sinc_arg = 0.16 * (tap_index - centre)
    safe_arg = np.where(sinc_arg == 0.0, 1.0, sinc_arg)
    sinc_vals = np.where(sinc_arg == 0.0, 1.0, np.sin(np.pi * safe_arg) / (np.pi * safe_arg))
    fir_taps = sinc_vals * hann_window
    fir_taps = fir_taps / fir_taps.sum()
    sample = np.arange(W)
    bin_index = np.arange(F)
    phase_grid = 2.0 * np.pi * np.outer(sample, bin_index) / W
    dft_table = np.concatenate([np.cos(phase_grid), -np.sin(phase_grid)], axis=1)
    combined = np.zeros((PAD + RAWW, 2 * F))
    for tap_number in range(TAPS):
        row_index = Q * sample - tap_number + PAD
        combined[row_index] += fir_taps[tap_number] * dft_table
    rising = np.sin(0.5 * np.pi * np.minimum(1.0, bin_index / 10.0)) ** 2
    falling = np.sin(0.5 * np.pi * np.minimum(1.0, (F - bin_index) / 16.0)) ** 2
    band_taper = rising * falling
    lag_index = np.arange(LAGS) - (LAGS - 1) / 2.0
    lag_phase = 2.0 * np.pi * np.outer(bin_index, lag_index) / W
    weight = np.where(bin_index == 0, 1.0, 2.0)[:, None]
    lag_table = np.stack([weight * np.cos(lag_phase), weight * np.sin(lag_phase)])
    table_hist = jnp.asarray(combined[:PAD], jnp.float32).astype(jnp.bfloat16)
    table_main = jnp.asarray(combined[PAD:], jnp.float32).astype(jnp.bfloat16)
    return (
        table_hist,
        table_main,
        jnp.asarray(band_taper, jnp.float32),
        jnp.asarray(lag_table, jnp.float32).astype(jnp.bfloat16),
    )


def whiten(spectrum, band_taper):
    amplitude = jnp.sqrt(spectrum[:, 0] * spectrum[:, 0] + spectrum[:, 1] * spectrum[:, 1])
    water_level = 0.5 * (jnp.mean(amplitude, axis=1, keepdims=True) + 1e-05)
    factor = band_taper[None, :, None] / jnp.maximum(amplitude, water_level)
    return (spectrum * factor[:, None]).astype(jnp.bfloat16)


def segment_terms(stacked_rows, partner, lag_table):
    cross_spec = jnp.einsum(
        "qwpfi,wpfj->fqij", stacked_rows, partner, preferred_element_type=jnp.float32
    ).astype(jnp.bfloat16)
    rows, columns = stacked_rows.shape[4], partner.shape[3]
    flat = cross_spec.reshape(2 * F, rows * columns)
    lag_flat = lag_table.transpose(1, 0, 2).reshape(2 * F, LAGS)
    terms = jnp.einsum("kn,kl->ln", flat, lag_flat, preferred_element_type=jnp.float32)
    return terms.astype(jnp.bfloat16).reshape(LAGS, rows, columns)


def per_device(raw_records, keep_window):
    channels_here = raw_records.shape[0]
    windows_here = keep_window.shape[0]
    segments = lax.axis_size(TM)
    blocks = lax.axis_size("chan")
    table_hist, table_main, band_taper, lag_table = make_tables()
    blocked = raw_records.reshape(channels_here, windows_here, RAWW)
    history = passed_along(raw_records[:, windows_here * RAWW - PAD :], TM, 1)
    previous = jnp.concatenate([history[:, None, :], blocked[:, :-1, RAWW - PAD :]], axis=1)
    spectrum = jnp.einsum("cwr,rq->wqc", blocked, table_main, preferred_element_type=jnp.float32)
    spectrum = spectrum + jnp.einsum(
        "cwr,rq->wqc", previous, table_hist, preferred_element_type=jnp.float32
    )
    whitened = whiten(spectrum.reshape(windows_here, 2, F, channels_here), band_taper)
    odd = [(b + 1, b) for b in range(0, blocks, 2)]
    partner_near = lax.ppermute(whitened, "chan", [((b + 1) % blocks, b) for b in range(blocks)])
    relayed = lax.ppermute(partner_near, "chan", odd)
    fetched = lax.ppermute(whitened, "chan", [((b + 2) % blocks, b) for b in range(1, blocks, 2)])
    is_odd = lax.axis_index("chan") % 2 == 1
    partner_far = jnp.where(is_odd, fetched, relayed)
    kept_spec = whitened * keep_window.astype(jnp.bfloat16)[:, None, None, None]
    rotated = jnp.stack([kept_spec[:, 1], -kept_spec[:, 0]], axis=1)
    stacked_rows = jnp.stack([kept_spec, rotated])
    terms = jnp.concatenate(
        [segment_terms(stacked_rows, partner, lag_table) for partner in (partner_near, partner_far)],
        axis=2,
    )
    columns = terms.shape[2]
    size_x, size_z = lax.axis_size("tx"), lax.axis_size("tz")
    row_count = channels_here // segments
    terms = terms.reshape(LAGS, size_x, size_z, row_count, columns).transpose(1, 2, 3, 0, 4)
    over_x = lax.all_to_all(terms, "tx", 0, 0, tiled=True)
    over_x = jnp.sum(over_x.astype(jnp.float32), axis=0).astype(jnp.bfloat16)
    over_z = lax.all_to_all(over_x, "tz", 0, 0, tiled=True)
    reduced = jnp.sum(over_z.astype(jnp.float32), axis=0)
    norm_factor = 1.0 / math.sqrt(windows_here * segments * F)
    return (reduced * norm_factor).astype(jnp.bfloat16)


def solution(mesh):
    chan_size, tm_size = mesh.devices.shape
    split_z = 4 if tm_size % 4 == 0 else 1
    grid = Mesh(mesh.devices.reshape(chan_size, tm_size // split_z, split_z), ("chan",) + TM)
    placed = (P("chan", TM), P(TM))
    return jax.shard_map(
        per_device,
        mesh=grid,
        in_specs=placed,
        out_specs=P(("chan",) + TM, None, None),
        check_vma=False,
    )
```

```python
import math

import jax
import jax.numpy as jnp
import numpy as np
from jax import lax
from jax.sharding import Mesh, PartitionSpec as P

W = 256
Q = 5
TAPS = 129
LAGS = 51
F = 128
RAWW = 1280
PAD = 128
TM = ("tx", "tz")


def passed_along(value, axis, by):
    devices = lax.axis_size(axis)
    pairs = [(i, i + by) for i in range(devices) if 0 <= i + by < devices]
    return lax.ppermute(value, axis, pairs)


def shifted(block, axis, distance):
    devices = range(lax.axis_size(axis))
    route = [((i - distance) % len(devices), i) for i in devices]
    return lax.ppermute(block, axis, route)


def make_tables():
    tap_index = np.arange(TAPS)
    centre = (TAPS - 1) / 2.0
    hann_window = 0.5 - 0.5 * np.cos(2.0 * np.pi * (tap_index + 1) / (TAPS + 1))
    sinc_arg = 0.16 * (tap_index - centre)
    safe_arg = np.where(sinc_arg == 0.0, 1.0, sinc_arg)
    sinc_vals = np.where(sinc_arg == 0.0, 1.0, np.sin(np.pi * safe_arg) / (np.pi * safe_arg))
    fir_taps = sinc_vals * hann_window
    fir_taps = fir_taps / fir_taps.sum()
    sample = np.arange(W)
    bin_index = np.arange(F)
    phase_grid = 2.0 * np.pi * np.outer(sample, bin_index) / W
    dft_table = np.concatenate([np.cos(phase_grid), -np.sin(phase_grid)], axis=1)
    combined = np.zeros((PAD + RAWW, 2 * F))
    for tap_number in range(TAPS):
        row_index = Q * sample - tap_number + PAD
        combined[row_index] += fir_taps[tap_number] * dft_table
    rising = np.sin(0.5 * np.pi * np.minimum(1.0, bin_index / 10.0)) ** 2
    falling = np.sin(0.5 * np.pi * np.minimum(1.0, (F - bin_index) / 16.0)) ** 2
    band_taper = rising * falling
    lag_index = np.arange(LAGS) - (LAGS - 1) / 2.0
    lag_phase = 2.0 * np.pi * np.outer(bin_index, lag_index) / W
    weight = np.where(bin_index == 0, 1.0, 2.0)[:, None]
    lag_table = np.stack([weight * np.cos(lag_phase), weight * np.sin(lag_phase)])
    table_hist = jnp.asarray(combined[:PAD], jnp.float32).astype(jnp.bfloat16)
    table_main = jnp.asarray(combined[PAD:], jnp.float32).astype(jnp.bfloat16)
    return (
        table_hist,
        table_main,
        jnp.asarray(band_taper, jnp.float32),
        jnp.asarray(lag_table, jnp.float32).astype(jnp.bfloat16),
    )


def whiten(spectrum, band_taper):
    amplitude = jnp.sqrt(spectrum[:, 0] * spectrum[:, 0] + spectrum[:, 1] * spectrum[:, 1])
    water_level = 0.5 * (jnp.mean(amplitude, axis=1, keepdims=True) + 1e-05)
    factor = band_taper[None, :, None] / jnp.maximum(amplitude, water_level)
    return (spectrum * factor[:, None]).astype(jnp.bfloat16)


def segment_terms(stacked_rows, partner, lag_table):
    cross_spec = jnp.einsum(
        "qwpfi,wpfj->fqij", stacked_rows, partner, preferred_element_type=jnp.float32
    ).astype(jnp.bfloat16)
    rows, columns = stacked_rows.shape[4], partner.shape[3]
    flat = cross_spec.reshape(2 * F, rows * columns)
    lag_flat = lag_table.transpose(1, 0, 2).reshape(2 * F, LAGS)
    terms = jnp.einsum("kn,kl->ln", flat, lag_flat, preferred_element_type=jnp.float32)
    return terms.astype(jnp.bfloat16).reshape(LAGS, rows, columns)


def per_device(raw_records, keep_window):
    channels_here = raw_records.shape[0]
    windows_here = keep_window.shape[0]
    segments = lax.axis_size(TM)
    blocks = lax.axis_size("chan")
    table_hist, table_main, band_taper, lag_table = make_tables()
    blocked = raw_records.reshape(channels_here, windows_here, RAWW)
    history = passed_along(raw_records[:, windows_here * RAWW - PAD :], TM, 1)
    previous = jnp.concatenate([history[:, None, :], blocked[:, :-1, RAWW - PAD :]], axis=1)
    spectrum = jnp.einsum("cwr,rq->wqc", blocked, table_main, preferred_element_type=jnp.float32)
    spectrum = spectrum + jnp.einsum(
        "cwr,rq->wqc", previous, table_hist, preferred_element_type=jnp.float32
    )
    whitened = whiten(spectrum.reshape(windows_here, 2, F, channels_here), band_taper)
    odd = [(b + 1, b) for b in range(0, blocks, 2)]
    partner_near = lax.ppermute(whitened, "chan", [((b + 1) % blocks, b) for b in range(blocks)])
    relayed = lax.ppermute(partner_near, "chan", odd)
    fetched = lax.ppermute(whitened, "chan", [((b + 2) % blocks, b) for b in range(1, blocks, 2)])
    is_odd = lax.axis_index("chan") % 2 == 1
    partner_far = jnp.where(is_odd, fetched, relayed)
    kept_spec = whitened * keep_window.astype(jnp.bfloat16)[:, None, None, None]
    rotated = jnp.stack([kept_spec[:, 1], -kept_spec[:, 0]], axis=1)
    stacked_rows = jnp.stack([kept_spec, rotated])
    terms = jnp.concatenate(
        [segment_terms(stacked_rows, partner, lag_table) for partner in (partner_near, partner_far)],
        axis=2,
    )
    columns = terms.shape[2]
    size_x, size_z = lax.axis_size("tx"), lax.axis_size("tz")
    row_count = channels_here // segments
    terms = terms.reshape(LAGS, size_x, size_z, row_count, columns).transpose(1, 2, 3, 0, 4)
    over_x = lax.all_to_all(terms, "tx", 0, 0, tiled=True)
    over_x = jnp.sum(over_x.astype(jnp.float32), axis=0).astype(jnp.bfloat16)
    over_z = lax.psum_scatter(
        over_x.reshape(size_z * row_count, LAGS * columns), "tz", scatter_dimension=0, tiled=True
    )
    reduced = over_z.reshape(row_count, LAGS, columns).astype(jnp.float32)
    norm_factor = 1.0 / math.sqrt(windows_here * segments * F)
    return (reduced * norm_factor).astype(jnp.bfloat16)


def solution(mesh):
    chan_size, tm_size = mesh.devices.shape
    split_z = 4 if tm_size % 4 == 0 else 1
    grid = Mesh(mesh.devices.reshape(chan_size, tm_size // split_z, split_z), ("chan",) + TM)
    placed = (P("chan", TM), P(TM))
    return jax.shard_map(
        per_device,
        mesh=grid,
        in_specs=placed,
        out_specs=P(("chan",) + TM, None, None),
        check_vma=False,
    )
```

```python
import math

import jax
import jax.numpy as jnp
import numpy as np
from jax import lax
from jax.sharding import Mesh, PartitionSpec as P

W = 256
Q = 5
TAPS = 129
LAGS = 51
F = 128
RAWW = 1280
PAD = 128
TM = ("tx", "tzh", "tzl")


def passed_along(value, axis, by):
    devices = lax.axis_size(axis)
    pairs = [(i, i + by) for i in range(devices) if 0 <= i + by < devices]
    return lax.ppermute(value, axis, pairs)


def shifted(block, axis, distance):
    devices = range(lax.axis_size(axis))
    route = [((i - distance) % len(devices), i) for i in devices]
    return lax.ppermute(block, axis, route)


def make_tables():
    tap_index = np.arange(TAPS)
    centre = (TAPS - 1) / 2.0
    hann_window = 0.5 - 0.5 * np.cos(2.0 * np.pi * (tap_index + 1) / (TAPS + 1))
    sinc_arg = 0.16 * (tap_index - centre)
    safe_arg = np.where(sinc_arg == 0.0, 1.0, sinc_arg)
    sinc_vals = np.where(sinc_arg == 0.0, 1.0, np.sin(np.pi * safe_arg) / (np.pi * safe_arg))
    fir_taps = sinc_vals * hann_window
    fir_taps = fir_taps / fir_taps.sum()
    sample = np.arange(W)
    bin_index = np.arange(F)
    phase_grid = 2.0 * np.pi * np.outer(sample, bin_index) / W
    dft_table = np.concatenate([np.cos(phase_grid), -np.sin(phase_grid)], axis=1)
    combined = np.zeros((PAD + RAWW, 2 * F))
    for tap_number in range(TAPS):
        row_index = Q * sample - tap_number + PAD
        combined[row_index] += fir_taps[tap_number] * dft_table
    rising = np.sin(0.5 * np.pi * np.minimum(1.0, bin_index / 10.0)) ** 2
    falling = np.sin(0.5 * np.pi * np.minimum(1.0, (F - bin_index) / 16.0)) ** 2
    band_taper = rising * falling
    lag_index = np.arange(LAGS) - (LAGS - 1) / 2.0
    lag_phase = 2.0 * np.pi * np.outer(bin_index, lag_index) / W
    weight = np.where(bin_index == 0, 1.0, 2.0)[:, None]
    lag_table = np.stack([weight * np.cos(lag_phase), weight * np.sin(lag_phase)])
    table_hist = jnp.asarray(combined[:PAD], jnp.float32).astype(jnp.bfloat16)
    table_main = jnp.asarray(combined[PAD:], jnp.float32).astype(jnp.bfloat16)
    return (
        table_hist,
        table_main,
        jnp.asarray(band_taper, jnp.float32),
        jnp.asarray(lag_table, jnp.float32).astype(jnp.bfloat16),
    )


def whiten(spectrum, band_taper):
    amplitude = jnp.sqrt(spectrum[:, 0] * spectrum[:, 0] + spectrum[:, 1] * spectrum[:, 1])
    water_level = 0.5 * (jnp.mean(amplitude, axis=1, keepdims=True) + 1e-05)
    factor = band_taper[None, :, None] / jnp.maximum(amplitude, water_level)
    return (spectrum * factor[:, None]).astype(jnp.bfloat16)


def segment_terms(stacked_rows, partner, lag_table):
    cross_spec = jnp.einsum(
        "qwpfi,wpfj->fqij", stacked_rows, partner, preferred_element_type=jnp.float32
    ).astype(jnp.bfloat16)
    rows, columns = stacked_rows.shape[4], partner.shape[3]
    flat = cross_spec.reshape(2 * F, rows * columns)
    lag_flat = lag_table.transpose(1, 0, 2).reshape(2 * F, LAGS)
    terms = jnp.einsum("kn,kl->ln", flat, lag_flat, preferred_element_type=jnp.float32)
    return terms.astype(jnp.bfloat16).reshape(LAGS, rows, columns)


def per_device(raw_records, keep_window):
    channels_here = raw_records.shape[0]
    windows_here = keep_window.shape[0]
    segments = lax.axis_size(TM)
    blocks = lax.axis_size("chan")
    table_hist, table_main, band_taper, lag_table = make_tables()
    blocked = raw_records.reshape(channels_here, windows_here, RAWW)
    history = passed_along(raw_records[:, windows_here * RAWW - PAD :], TM, 1)
    previous = jnp.concatenate([history[:, None, :], blocked[:, :-1, RAWW - PAD :]], axis=1)
    spectrum = jnp.einsum("cwr,rq->wqc", blocked, table_main, preferred_element_type=jnp.float32)
    spectrum = spectrum + jnp.einsum(
        "cwr,rq->wqc", previous, table_hist, preferred_element_type=jnp.float32
    )
    whitened = whiten(spectrum.reshape(windows_here, 2, F, channels_here), band_taper)
    odd = [(b + 1, b) for b in range(0, blocks, 2)]
    partner_near = lax.ppermute(whitened, "chan", [((b + 1) % blocks, b) for b in range(blocks)])
    relayed = lax.ppermute(partner_near, "chan", odd)
    fetched = lax.ppermute(whitened, "chan", [((b + 2) % blocks, b) for b in range(1, blocks, 2)])
    is_odd = lax.axis_index("chan") % 2 == 1
    partner_far = jnp.where(is_odd, fetched, relayed)
    kept_spec = whitened * keep_window.astype(jnp.bfloat16)[:, None, None, None]
    rotated = jnp.stack([kept_spec[:, 1], -kept_spec[:, 0]], axis=1)
    stacked_rows = jnp.stack([kept_spec, rotated])
    terms = jnp.concatenate(
        [segment_terms(stacked_rows, partner, lag_table) for partner in (partner_near, partner_far)],
        axis=2,
    )
    columns = terms.shape[2]
    size_x, size_z = lax.axis_size("tx"), lax.axis_size(("tzh", "tzl"))
    row_count = channels_here // segments
    terms = terms.reshape(LAGS, size_x, size_z, row_count, columns).transpose(1, 2, 3, 0, 4)
    over_x = lax.all_to_all(terms, "tx", 0, 0, tiled=True)
    over_x = jnp.sum(over_x.astype(jnp.float32), axis=0).astype(jnp.bfloat16)
    pair = lax.axis_size("tzl")
    over_x = over_x.reshape((size_z // pair, pair) + over_x.shape[1:])
    over_near = lax.all_to_all(over_x, "tzl", 1, 1, tiled=True)
    over_near = jnp.sum(over_near.astype(jnp.float32), axis=1).astype(jnp.bfloat16)
    over_far = lax.all_to_all(over_near, "tzh", 0, 0, tiled=True)
    reduced = jnp.sum(over_far.astype(jnp.float32), axis=0)
    norm_factor = 1.0 / math.sqrt(windows_here * segments * F)
    return (reduced * norm_factor).astype(jnp.bfloat16)


def solution(mesh):
    chan_size, tm_size = mesh.devices.shape
    split_z = 4 if tm_size % 4 == 0 else 1
    grid = Mesh(
        mesh.devices.reshape(chan_size, tm_size // split_z, split_z // 2, 2), ("chan",) + TM
    )
    placed = (P("chan", TM), P(TM))
    return jax.shard_map(
        per_device,
        mesh=grid,
        in_specs=placed,
        out_specs=P(("chan",) + TM, None, None),
        check_vma=False,
    )
```

```python
import math

import jax
import jax.numpy as jnp
import numpy as np
from jax import lax
from jax.sharding import Mesh, PartitionSpec as P

W = 256
Q = 5
TAPS = 129
LAGS = 51
F = 128
RAWW = 1280
PAD = 128
TM = ("tx", "tzh", "tzl")


def passed_along(value, axis, by):
    devices = lax.axis_size(axis)
    pairs = [(i, i + by) for i in range(devices) if 0 <= i + by < devices]
    return lax.ppermute(value, axis, pairs)


def shifted(block, axis, distance):
    devices = range(lax.axis_size(axis))
    route = [((i - distance) % len(devices), i) for i in devices]
    return lax.ppermute(block, axis, route)


def make_tables():
    tap_index = np.arange(TAPS)
    centre = (TAPS - 1) / 2.0
    hann_window = 0.5 - 0.5 * np.cos(2.0 * np.pi * (tap_index + 1) / (TAPS + 1))
    sinc_arg = 0.16 * (tap_index - centre)
    safe_arg = np.where(sinc_arg == 0.0, 1.0, sinc_arg)
    sinc_vals = np.where(sinc_arg == 0.0, 1.0, np.sin(np.pi * safe_arg) / (np.pi * safe_arg))
    fir_taps = sinc_vals * hann_window
    fir_taps = fir_taps / fir_taps.sum()
    sample = np.arange(W)
    bin_index = np.arange(F)
    phase_grid = 2.0 * np.pi * np.outer(sample, bin_index) / W
    dft_table = np.concatenate([np.cos(phase_grid), -np.sin(phase_grid)], axis=1)
    combined = np.zeros((PAD + RAWW, 2 * F))
    for tap_number in range(TAPS):
        row_index = Q * sample - tap_number + PAD
        combined[row_index] += fir_taps[tap_number] * dft_table
    rising = np.sin(0.5 * np.pi * np.minimum(1.0, bin_index / 10.0)) ** 2
    falling = np.sin(0.5 * np.pi * np.minimum(1.0, (F - bin_index) / 16.0)) ** 2
    band_taper = rising * falling
    lag_index = np.arange(LAGS) - (LAGS - 1) / 2.0
    lag_phase = 2.0 * np.pi * np.outer(bin_index, lag_index) / W
    weight = np.where(bin_index == 0, 1.0, 2.0)[:, None]
    lag_table = np.stack([weight * np.cos(lag_phase), weight * np.sin(lag_phase)])
    table_hist = jnp.asarray(combined[:PAD], jnp.float32).astype(jnp.bfloat16)
    table_main = jnp.asarray(combined[PAD:], jnp.float32).astype(jnp.bfloat16)
    return (
        table_hist,
        table_main,
        jnp.asarray(band_taper, jnp.float32),
        jnp.asarray(lag_table, jnp.float32).astype(jnp.bfloat16),
    )


def whiten(spectrum, band_taper):
    amplitude = jnp.sqrt(spectrum[:, 0] * spectrum[:, 0] + spectrum[:, 1] * spectrum[:, 1])
    water_level = 0.5 * (jnp.mean(amplitude, axis=1, keepdims=True) + 1e-05)
    factor = band_taper[None, :, None] / jnp.maximum(amplitude, water_level)
    return (spectrum * factor[:, None]).astype(jnp.bfloat16)


def segment_terms(stacked_rows, partner, lag_table):
    cross_spec = jnp.einsum(
        "qwpfi,wpfj->fqij", stacked_rows, partner, preferred_element_type=jnp.float32
    ).astype(jnp.bfloat16)
    rows, columns = stacked_rows.shape[4], partner.shape[3]
    flat = cross_spec.reshape(2 * F, rows * columns)
    lag_flat = lag_table.transpose(1, 0, 2).reshape(2 * F, LAGS)
    terms = jnp.einsum("kn,kl->ln", flat, lag_flat, preferred_element_type=jnp.float32)
    return terms.astype(jnp.bfloat16).reshape(LAGS, rows, columns)


def per_device(raw_records, keep_window):
    channels_here = raw_records.shape[0]
    windows_here = keep_window.shape[0]
    segments = lax.axis_size(TM)
    blocks = lax.axis_size("chan")
    table_hist, table_main, band_taper, lag_table = make_tables()
    blocked = raw_records.reshape(channels_here, windows_here, RAWW)
    history = passed_along(raw_records[:, windows_here * RAWW - PAD :], TM, 1)
    previous = jnp.concatenate([history[:, None, :], blocked[:, :-1, RAWW - PAD :]], axis=1)
    spectrum = jnp.einsum("cwr,rq->wqc", blocked, table_main, preferred_element_type=jnp.float32)
    spectrum = spectrum + jnp.einsum(
        "cwr,rq->wqc", previous, table_hist, preferred_element_type=jnp.float32
    )
    whitened = whiten(spectrum.reshape(windows_here, 2, F, channels_here), band_taper)
    odd = [(b + 1, b) for b in range(0, blocks, 2)]
    partner_near = lax.ppermute(whitened, "chan", [((b + 1) % blocks, b) for b in range(blocks)])
    relayed = lax.ppermute(partner_near, "chan", odd)
    fetched = lax.ppermute(whitened, "chan", [((b + 2) % blocks, b) for b in range(1, blocks, 2)])
    is_odd = lax.axis_index("chan") % 2 == 1
    partner_far = jnp.where(is_odd, fetched, relayed)
    kept_spec = whitened * keep_window.astype(jnp.bfloat16)[:, None, None, None]
    rotated = jnp.stack([kept_spec[:, 1], -kept_spec[:, 0]], axis=1)
    stacked_rows = jnp.stack([kept_spec, rotated])
    terms = jnp.concatenate(
        [segment_terms(stacked_rows, partner, lag_table) for partner in (partner_near, partner_far)],
        axis=2,
    )
    columns = terms.shape[2]
    size_x, size_z = lax.axis_size("tx"), lax.axis_size(("tzh", "tzl"))
    row_count = channels_here // segments
    terms = terms.reshape(LAGS, size_x, size_z, row_count, columns).transpose(1, 2, 3, 0, 4)
    pair = lax.axis_size("tzl")
    halves = size_z // pair
    grouped = terms.reshape((size_x, halves, pair) + terms.shape[2:]).transpose(0, 2, 1, 3, 4, 5)
    grouped = grouped.reshape((size_x * pair, halves) + terms.shape[2:])
    over_first = lax.all_to_all(grouped, ("tx", "tzl"), 0, 0, tiled=True)
    over_first = jnp.sum(over_first.astype(jnp.float32), axis=0).astype(jnp.bfloat16)
    over_far = lax.all_to_all(over_first, "tzh", 0, 0, tiled=True)
    reduced = jnp.sum(over_far.astype(jnp.float32), axis=0)
    norm_factor = 1.0 / math.sqrt(windows_here * segments * F)
    return (reduced * norm_factor).astype(jnp.bfloat16)


def solution(mesh):
    chan_size, tm_size = mesh.devices.shape
    split_z = 4 if tm_size % 4 == 0 else 1
    grid = Mesh(
        mesh.devices.reshape(chan_size, tm_size // split_z, split_z // 2, 2), ("chan",) + TM
    )
    placed = (P("chan", TM), P(TM))
    return jax.shard_map(
        per_device,
        mesh=grid,
        in_specs=placed,
        out_specs=P(("chan",) + TM, None, None),
        check_vma=False,
    )
```

```python
import math

import jax
import jax.numpy as jnp
import numpy as np
from jax import lax
from jax.sharding import Mesh, PartitionSpec as P

W = 256
Q = 5
TAPS = 129
LAGS = 51
F = 128
RAWW = 1280
PAD = 128
TM = ("tx", "tzh", "tzl")


def passed_along(value, axis, by):
    devices = lax.axis_size(axis)
    pairs = [(i, i + by) for i in range(devices) if 0 <= i + by < devices]
    return lax.ppermute(value, axis, pairs)


def shifted(block, axis, distance):
    devices = range(lax.axis_size(axis))
    route = [((i - distance) % len(devices), i) for i in devices]
    return lax.ppermute(block, axis, route)


def make_tables():
    tap_index = np.arange(TAPS)
    centre = (TAPS - 1) / 2.0
    hann_window = 0.5 - 0.5 * np.cos(2.0 * np.pi * (tap_index + 1) / (TAPS + 1))
    sinc_arg = 0.16 * (tap_index - centre)
    safe_arg = np.where(sinc_arg == 0.0, 1.0, sinc_arg)
    sinc_vals = np.where(sinc_arg == 0.0, 1.0, np.sin(np.pi * safe_arg) / (np.pi * safe_arg))
    fir_taps = sinc_vals * hann_window
    fir_taps = fir_taps / fir_taps.sum()
    sample = np.arange(W)
    bin_index = np.arange(F)
    phase_grid = 2.0 * np.pi * np.outer(sample, bin_index) / W
    dft_table = np.concatenate([np.cos(phase_grid), -np.sin(phase_grid)], axis=1)
    combined = np.zeros((PAD + RAWW, 2 * F))
    for tap_number in range(TAPS):
        row_index = Q * sample - tap_number + PAD
        combined[row_index] += fir_taps[tap_number] * dft_table
    rising = np.sin(0.5 * np.pi * np.minimum(1.0, bin_index / 10.0)) ** 2
    falling = np.sin(0.5 * np.pi * np.minimum(1.0, (F - bin_index) / 16.0)) ** 2
    band_taper = rising * falling
    lag_index = np.arange(LAGS) - (LAGS - 1) / 2.0
    lag_phase = 2.0 * np.pi * np.outer(bin_index, lag_index) / W
    weight = np.where(bin_index == 0, 1.0, 2.0)[:, None]
    lag_table = np.stack([weight * np.cos(lag_phase), weight * np.sin(lag_phase)])
    table_hist = jnp.asarray(combined[:PAD], jnp.float32).astype(jnp.bfloat16)
    table_main = jnp.asarray(combined[PAD:], jnp.float32).astype(jnp.bfloat16)
    return (
        table_hist,
        table_main,
        jnp.asarray(band_taper, jnp.float32),
        jnp.asarray(lag_table, jnp.float32).astype(jnp.bfloat16),
    )


def whiten(spectrum, band_taper):
    amplitude = jnp.sqrt(spectrum[:, 0] * spectrum[:, 0] + spectrum[:, 1] * spectrum[:, 1])
    water_level = 0.5 * (jnp.mean(amplitude, axis=1, keepdims=True) + 1e-05)
    factor = band_taper[None, :, None] / jnp.maximum(amplitude, water_level)
    return (spectrum * factor[:, None]).astype(jnp.bfloat16)


def segment_terms(stacked_rows, partner, lag_table):
    cross_spec = jnp.einsum(
        "qwpfi,wpfj->fqij", stacked_rows, partner, preferred_element_type=jnp.float32
    ).astype(jnp.bfloat16)
    rows, columns = stacked_rows.shape[4], partner.shape[3]
    flat = cross_spec.reshape(2 * F, rows * columns)
    lag_flat = lag_table.transpose(1, 0, 2).reshape(2 * F, LAGS)
    terms = jnp.einsum("kn,kl->ln", flat, lag_flat, preferred_element_type=jnp.float32)
    return terms.astype(jnp.bfloat16).reshape(LAGS, rows, columns)


def per_device(raw_records, keep_window):
    channels_here = raw_records.shape[0]
    windows_here = keep_window.shape[0]
    segments = lax.axis_size(TM)
    blocks = lax.axis_size("chan")
    table_hist, table_main, band_taper, lag_table = make_tables()
    blocked = raw_records.reshape(channels_here, windows_here, RAWW)
    history = passed_along(raw_records[:, windows_here * RAWW - PAD :], TM, 1)
    previous = jnp.concatenate([history[:, None, :], blocked[:, :-1, RAWW - PAD :]], axis=1)
    spectrum = jnp.einsum("cwr,rq->wqc", blocked, table_main, preferred_element_type=jnp.float32)
    spectrum = spectrum + jnp.einsum(
        "cwr,rq->wqc", previous, table_hist, preferred_element_type=jnp.float32
    )
    whitened = whiten(spectrum.reshape(windows_here, 2, F, channels_here), band_taper)
    odd = [(b + 1, b) for b in range(0, blocks, 2)]
    partner_near = lax.ppermute(whitened, "chan", [((b + 1) % blocks, b) for b in range(blocks)])
    relayed = lax.ppermute(partner_near, "chan", odd)
    fetched = lax.ppermute(whitened, "chan", [((b + 2) % blocks, b) for b in range(1, blocks, 2)])
    is_odd = lax.axis_index("chan") % 2 == 1
    partner_far = jnp.where(is_odd, fetched, relayed)
    kept_spec = whitened * keep_window.astype(jnp.bfloat16)[:, None, None, None]
    rotated = jnp.stack([kept_spec[:, 1], -kept_spec[:, 0]], axis=1)
    stacked_rows = jnp.stack([kept_spec, rotated])
    terms = jnp.concatenate(
        [segment_terms(stacked_rows, partner, lag_table) for partner in (partner_near, partner_far)],
        axis=2,
    )
    columns = terms.shape[2]
    size_x, size_z = lax.axis_size("tx"), lax.axis_size(("tzh", "tzl"))
    row_count = channels_here // segments
    terms = terms.reshape(LAGS, size_x, size_z, row_count, columns).transpose(1, 2, 3, 0, 4)
    pair = lax.axis_size("tzl")
    halves = size_z // pair
    grouped = terms.reshape((size_x, halves, pair) + terms.shape[2:]).transpose(0, 2, 1, 3, 4, 5)
    grouped = grouped.reshape((size_x * pair, halves) + terms.shape[2:])
    over_first = lax.all_to_all(grouped, ("tx", "tzl"), 0, 0, tiled=True)
    over_first = jnp.sum(over_first.astype(jnp.float32), axis=0).astype(jnp.bfloat16)
    here = lax.axis_index("tzh")
    kept = lax.dynamic_index_in_dim(over_first, here, 0, keepdims=False)
    given = lax.dynamic_index_in_dim(over_first, halves - 1 - here, 0, keepdims=False)
    received = lax.ppermute(given, "tzh", [(h, halves - 1 - h) for h in range(halves)])
    reduced = kept.astype(jnp.float32) + received.astype(jnp.float32)
    norm_factor = 1.0 / math.sqrt(windows_here * segments * F)
    return (reduced * norm_factor).astype(jnp.bfloat16)


def solution(mesh):
    chan_size, tm_size = mesh.devices.shape
    split_z = 4 if tm_size % 4 == 0 else 1
    grid = Mesh(
        mesh.devices.reshape(chan_size, tm_size // split_z, split_z // 2, 2), ("chan",) + TM
    )
    placed = (P("chan", TM), P(TM))
    return jax.shard_map(
        per_device,
        mesh=grid,
        in_specs=placed,
        out_specs=P(("chan",) + TM, None, None),
        check_vma=False,
    )
```

```python
import math

import jax
import jax.numpy as jnp
import numpy as np
from jax import lax
from jax.sharding import Mesh, PartitionSpec as P

W = 256
Q = 5
TAPS = 129
LAGS = 51
F = 128
RAWW = 1280
PAD = 128
TM = ("tx", "tzh", "tzl")


def passed_along(value, axis, by):
    devices = lax.axis_size(axis)
    pairs = [(i, i + by) for i in range(devices) if 0 <= i + by < devices]
    return lax.ppermute(value, axis, pairs)


def shifted(block, axis, distance):
    devices = range(lax.axis_size(axis))
    route = [((i - distance) % len(devices), i) for i in devices]
    return lax.ppermute(block, axis, route)


def make_tables():
    tap_index = np.arange(TAPS)
    centre = (TAPS - 1) / 2.0
    hann_window = 0.5 - 0.5 * np.cos(2.0 * np.pi * (tap_index + 1) / (TAPS + 1))
    sinc_arg = 0.16 * (tap_index - centre)
    safe_arg = np.where(sinc_arg == 0.0, 1.0, sinc_arg)
    sinc_vals = np.where(sinc_arg == 0.0, 1.0, np.sin(np.pi * safe_arg) / (np.pi * safe_arg))
    fir_taps = sinc_vals * hann_window
    fir_taps = fir_taps / fir_taps.sum()
    sample = np.arange(W)
    bin_index = np.arange(F)
    phase_grid = 2.0 * np.pi * np.outer(sample, bin_index) / W
    dft_table = np.concatenate([np.cos(phase_grid), -np.sin(phase_grid)], axis=1)
    combined = np.zeros((PAD + RAWW, 2 * F))
    for tap_number in range(TAPS):
        row_index = Q * sample - tap_number + PAD
        combined[row_index] += fir_taps[tap_number] * dft_table
    rising = np.sin(0.5 * np.pi * np.minimum(1.0, bin_index / 10.0)) ** 2
    falling = np.sin(0.5 * np.pi * np.minimum(1.0, (F - bin_index) / 16.0)) ** 2
    band_taper = rising * falling
    lag_index = np.arange(LAGS) - (LAGS - 1) / 2.0
    lag_phase = 2.0 * np.pi * np.outer(bin_index, lag_index) / W
    weight = np.where(bin_index == 0, 1.0, 2.0)[:, None]
    lag_table = np.stack([weight * np.cos(lag_phase), weight * np.sin(lag_phase)])
    table_hist = jnp.asarray(combined[:PAD], jnp.float32).astype(jnp.bfloat16)
    table_main = jnp.asarray(combined[PAD:], jnp.float32).astype(jnp.bfloat16)
    return (
        table_hist,
        table_main,
        jnp.asarray(band_taper, jnp.float32),
        jnp.asarray(lag_table, jnp.float32).astype(jnp.bfloat16),
    )


def whiten(spectrum, band_taper):
    amplitude = jnp.sqrt(spectrum[:, 0] * spectrum[:, 0] + spectrum[:, 1] * spectrum[:, 1])
    water_level = 0.5 * (jnp.mean(amplitude, axis=1, keepdims=True) + 1e-05)
    factor = band_taper[None, :, None] / jnp.maximum(amplitude, water_level)
    return (spectrum * factor[:, None]).astype(jnp.bfloat16)


def segment_terms(stacked_rows, partner, lag_table):
    cross_spec = jnp.einsum(
        "qwpfi,wpfj->fqij", stacked_rows, partner, preferred_element_type=jnp.float32
    ).astype(jnp.bfloat16)
    rows, columns = stacked_rows.shape[4], partner.shape[3]
    flat = cross_spec.reshape(2 * F, rows * columns)
    lag_flat = lag_table.transpose(1, 0, 2).reshape(2 * F, LAGS)
    terms = jnp.einsum("kn,kl->ln", flat, lag_flat, preferred_element_type=jnp.float32)
    return terms.astype(jnp.bfloat16).reshape(LAGS, rows, columns)


def per_device(raw_records, keep_window):
    channels_here = raw_records.shape[0]
    windows_here = keep_window.shape[0]
    segments = lax.axis_size(TM)
    blocks = lax.axis_size("chan")
    table_hist, table_main, band_taper, lag_table = make_tables()
    blocked = raw_records.reshape(channels_here, windows_here, RAWW)
    history = passed_along(raw_records[:, windows_here * RAWW - PAD :], TM, 1)
    previous = jnp.concatenate([history[:, None, :], blocked[:, :-1, RAWW - PAD :]], axis=1)
    spectrum = jnp.einsum("cwr,rq->wqc", blocked, table_main, preferred_element_type=jnp.float32)
    spectrum = spectrum + jnp.einsum(
        "cwr,rq->wqc", previous, table_hist, preferred_element_type=jnp.float32
    )
    whitened = whiten(spectrum.reshape(windows_here, 2, F, channels_here), band_taper)
    odd = [(b + 1, b) for b in range(0, blocks, 2)]
    partner_near = lax.ppermute(whitened, "chan", [((b + 1) % blocks, b) for b in range(blocks)])
    relayed = lax.ppermute(partner_near, "chan", odd)
    fetched = lax.ppermute(whitened, "chan", [((b + 2) % blocks, b) for b in range(1, blocks, 2)])
    is_odd = lax.axis_index("chan") % 2 == 1
    partner_far = jnp.where(is_odd, fetched, relayed)
    kept_spec = whitened * keep_window.astype(jnp.bfloat16)[:, None, None, None]
    rotated = jnp.stack([kept_spec[:, 1], -kept_spec[:, 0]], axis=1)
    stacked_rows = jnp.stack([kept_spec, rotated])
    terms = jnp.concatenate(
        [segment_terms(stacked_rows, partner, lag_table) for partner in (partner_near, partner_far)],
        axis=2,
    )
    columns = terms.shape[2]
    size_x, size_z = lax.axis_size("tx"), lax.axis_size(("tzh", "tzl"))
    row_count = channels_here // segments
    terms = terms.reshape(LAGS, size_x, size_z, row_count, columns).transpose(1, 2, 3, 0, 4)
    pair = lax.axis_size("tzl")
    halves = size_z // pair
    grouped = terms.reshape((size_x, halves, pair) + terms.shape[2:]).transpose(2, 0, 1, 3, 4, 5)
    grouped = grouped.reshape((pair * size_x, halves) + terms.shape[2:])
    over_first = lax.all_to_all(grouped, ("tzl", "tx"), 0, 0, tiled=True)
    over_first = jnp.sum(over_first.astype(jnp.float32), axis=0).astype(jnp.bfloat16)
    over_far = lax.all_to_all(over_first, "tzh", 0, 0, tiled=True)
    reduced = jnp.sum(over_far.astype(jnp.float32), axis=0)
    norm_factor = 1.0 / math.sqrt(windows_here * segments * F)
    return (reduced * norm_factor).astype(jnp.bfloat16)


def solution(mesh):
    chan_size, tm_size = mesh.devices.shape
    split_z = 4 if tm_size % 4 == 0 else 1
    grid = Mesh(
        mesh.devices.reshape(chan_size, tm_size // split_z, split_z // 2, 2), ("chan",) + TM
    )
    placed = (P("chan", TM), P(TM))
    return jax.shard_map(
        per_device,
        mesh=grid,
        in_specs=placed,
        out_specs=P(("chan",) + TM, None, None),
        check_vma=False,
    )
```
